256 devices in a mesh: dp: 8 (over x, core), expert: 32 (over y, z).
Axes of the slice: x: 4, y: 4, z: 8, core: 2. Of those that a mesh axis runs over, the one named last changes fastest.
Arguments:
- tokens: bfloat16 [12288, 2048], P(('dp', 'expert')), may hold values from -6 to 6
- routes: int32 [12288, 6], P(('dp', 'expert')), may hold values from 0 to 31, all different within a row; in each aligned block of 48 rows (0 to 47, 48 to 95, ...) at most 12 rows name the same one
- gates: float32 [12288, 6], P(('dp', 'expert')), may hold values from 0.02 to 0.5
- cotangent: bfloat16 [12288, 2048], P(('dp', 'expert')), may hold values from -6 to 6
- swap_flag: int32 [32], replicated, may hold values from 0 to 1, as said below
- w_up: bfloat16 [32, 2048, 1408], P('expert', 'dp'), may hold values from -0.125 to 0.125
- w_down: bfloat16 [32, 1408, 2048], P('expert', 'dp'), may hold values from -0.15625 to 0.15625
- m_up: bfloat16 [32, 2048, 1408], P('expert', 'dp'), may hold values from -12 to 12
- v_up: bfloat16 [32, 2048, 1408], P('expert', 'dp'), may hold values from 1 to 50
- m_down: bfloat16 [32, 1408, 2048], P('expert', 'dp'), may hold values from -12 to 12
- v_down: bfloat16 [32, 1408, 2048], P('expert', 'dp'), may hold values from 1 to 50
Outputs:
- mixed: bfloat16 [12288, 2048], P(('dp', 'expert'))
- input_grad: bfloat16 [12288, 2048], P(('dp', 'expert'))
- new_w_up: bfloat16 [32, 2048, 1408], P('expert', 'dp')
- new_w_down: bfloat16 [32, 1408, 2048], P('expert', 'dp')
- new_m_up: bfloat16 [32, 2048, 1408], P('expert', 'dp')
- new_v_up: bfloat16 [32, 2048, 1408], P('expert', 'dp')
- new_m_down: bfloat16 [32, 1408, 2048], P('expert', 'dp')
- new_v_down: bfloat16 [32, 1408, 2048], P('expert', 'dp')
The draws below stay inside these ranges and needn't reach their ends.
Inputs may be any that keep to these rules, and one draw needn't show every extreme that they name: `routes`: in each aligned block of 48 rows (the tokens of one device) no expert is chosen by more than 12 rows, a bound that some block reaches; the 6 experts of a row differ. swap_flag[e] == swap_flag[e xor 1] for every e; the pairs of experts 0 and 2 * (8) trade places in every draw, and some other pair stays.
All inputs are finite; a program needn't handle non-finite values.
Results may differ from the reference program's by a relative error of at most 0.015.
Values may be sent and summed in bfloat16 or wider, within the bound.
No kernel may reach another device: no remote copies, remote signals or barrier semaphores. Data moves between devices by JAX's collectives and lax.ppermute only.
A program may use at most 128 MiB of HBM per device.

```python
import math
import jax
import jax.numpy as jnp
import numpy as np
from jax import lax

D = 2048
FF = 1408
TOP = 6
TOK_DEV = 48
ADAM_STEP = 10
EXPERTS = 32
CAP = 12
TOKENS = 12288
N_DP = 8
N_EXPERT = 32


def draw_swap_flag(key, part):
    pair_count = EXPERTS // 2
    quarter = EXPERTS // 4
    key_one, key_two = jax.random.split(key)
    pair_bits = jax.random.randint(key_one, (pair_count,), 0, 2)
    staying = jax.random.randint(key_two, (), quarter + 1, pair_count)
    pair_bits = pair_bits.at[0].set(1).at[quarter].set(1).at[staying].set(0)
    return jnp.repeat(pair_bits, 2).astype(jnp.int32)


def levels(key, extent, shards, low, high):
    def one(axis_at, blocks):
        steps = jax.random.uniform(jax.random.fold_in(jax.random.fold_in(key, 6), axis_at), (blocks,), jnp.float32, low / len(shards), high / len(shards))
        return jnp.repeat(jnp.exp(steps), extent[axis_at] // blocks).reshape((-1,) + (1,) * (len(extent) - axis_at - 1))

    level = one(*shards[0])
    for cut in shards[1:]:
        level = level * one(*cut)
    return level


def deal_out(rng, own, number, rows, count, top, most, lean):
    sequence = jax.random.permutation(rng, count)
    crowded, usual = shares(count, rows * top, most, lean, True), shares(count, rows * top, most, lean, False)
    places = jnp.arange(count)

    def named(tallies, offset_by):
        used = int((tallies > 0).sum())
        fixed = max(1, used // 4)
        passed = fixed + (places - fixed + offset_by * (used - fixed)) % max(1, count - fixed)
        return jnp.zeros((count,), jnp.int32).at[sequence[jnp.where(places < fixed, places, passed)]].set(jnp.asarray(tallies, jnp.int32))

    tallies = jnp.where(number % 4 == 0, named(crowded, number // 4), named(usual, number - number // 4 - 1))
    mixed = jax.random.permutation(jax.random.fold_in(own, 3), count)
    donor, taker = mixed[0:count // 2 * 2:2], mixed[1:count // 2 * 2:2]
    margin = jnp.minimum(tallies[donor] - 1, most - tallies[taker]) // 2
    margin = jnp.where((donor == sequence[0]) | (taker == sequence[0]) | (tallies[taker] == 0), 0, jnp.maximum(margin, 0))
    passed = jax.random.randint(jax.random.fold_in(own, 4), (count // 2,), 0, 1 << 20) % (margin + 1)
    tallies = tallies.at[donor].add(-passed).at[taker].add(passed)
    labels = jnp.searchsorted(jnp.cumsum(tallies), jnp.arange(rows * top), side="right").astype(jnp.int32)
    listing = labels.reshape(top, rows).T
    listing = listing[jax.random.permutation(jax.random.fold_in(own, 1), rows)]
    offset_by = jax.random.randint(jax.random.fold_in(own, 2), (rows, 1), 0, top)
    return jnp.take_along_axis(listing, (jnp.arange(top)[None, :] + offset_by) % top, axis=1)


def shares(number_of, total, reach, skew, full):
    loads = [(1 << 20) // math.isqrt(standing ** skew) + 1 for standing in range(1, number_of + 1)]
    largest = reach if full else min(reach, max(-(-total // number_of), total * loads[0] // sum(loads)))
    least = 1 if total - largest >= number_of - 1 else 0
    given, rest = [largest] + [least] * (number_of - 1), total - largest - least * (number_of - 1)
    while rest > 0:
        movable = [i for i in range(1, number_of) if given[i] < largest] or [i for i in range(1, number_of) if given[i] < reach]
        mass, budget = sum([loads[i] for i in movable]), rest
        for i in movable:
            extra = min(reach - given[i], max(1, budget * loads[i] // mass), rest)
            given[i] = given[i] + extra
            rest = rest - extra
    return np.array(given)


def gaussian(own_key, shape, width, most, cuts=(), held_as=jnp.bfloat16):
    array = width * jax.random.normal(own_key, shape, jnp.float32)
    if cuts:
        array = array * levels(own_key, shape, cuts, -0.22, 0.18)
    return jnp.clip(array, -most, most).astype(held_as)


def setup_inputs(seed: int = 0) -> dict:
    key_of = jax.random.split(jax.random.key(seed), 12)
    tokens = gaussian(key_of[0], (TOKENS, D), 1.0, 6.0, ((0, 256),))
    routes_keys = jax.random.split(jax.random.fold_in(key_of[1], 1), TOKENS // TOK_DEV)
    routes_turns = jax.random.permutation(jax.random.fold_in(key_of[1], 3), TOKENS // TOK_DEV)
    routes = jax.vmap(lambda own, number: deal_out(jax.random.fold_in(key_of[1], 2), own, number, TOK_DEV, EXPERTS, TOP, CAP, 2))(routes_keys, routes_turns).reshape((TOKENS, TOP))
    gates = jnp.clip(jnp.exp(math.log(0.5) - 3.218876 * jax.random.uniform(key_of[2], (TOKENS, TOP), jnp.float32) ** levels(key_of[2], (TOKENS, TOP), ((0, 256),), -0.2, 0.2)), 0.02, 0.5)
    cotangent = gaussian(key_of[3], (TOKENS, D), 1.0, 6.0, ((0, 256),))
    swap_flag = draw_swap_flag(jax.random.fold_in(key_of[11], 71), 0)
    w_up = gaussian(key_of[5], (EXPERTS, D, FF), D ** -0.5, 0.125, ((0, 32), (1, 8)))
    w_down = gaussian(key_of[6], (EXPERTS, FF, D), FF ** -0.5, 0.15625, ((0, 32), (1, 8)))
    m_up = gaussian(key_of[7], (EXPERTS, D, FF), 2.0, 12.0, ((0, 32), (1, 8)))
    v_up = jnp.clip(jnp.exp(math.log(50.0) - 3.912023 * jax.random.uniform(key_of[8], (EXPERTS, D, FF), jnp.float32) ** levels(key_of[8], (EXPERTS, D, FF), ((0, 32), (1, 8)), -0.2, 0.2)), 1.0, 50.0).astype(jnp.bfloat16)
    m_down = gaussian(key_of[9], (EXPERTS, FF, D), 2.0, 12.0, ((0, 32), (1, 8)))
    v_down = jnp.clip(jnp.exp(math.log(50.0) - 3.912023 * jax.random.uniform(key_of[10], (EXPERTS, FF, D), jnp.float32) ** levels(key_of[10], (EXPERTS, FF, D), ((0, 32), (1, 8)), -0.2, 0.2)), 1.0, 50.0).astype(jnp.bfloat16)
    return {"tokens": tokens, "routes": routes, "gates": gates, "cotangent": cotangent, "swap_flag": swap_flag, "w_up": w_up, "w_down": w_down, "m_up": m_up, "v_up": v_up, "m_down": m_down, "v_down": v_down}


beta_one = 0.9
beta_two = 0.95
learn_rate = 0.001
adam_eps = 1e-08

def silu_slope(value):
    sigma = jax.nn.sigmoid(value)
    return sigma * (1.0 + value * (1.0 - sigma))

def adam_update(weight, first_moment, second_moment, gradient):
    first_new = beta_one * first_moment.astype(jnp.float32) + (1.0 - beta_one) * gradient
    second_new = beta_two * second_moment.astype(jnp.float32) + (1.0 - beta_two) * gradient * gradient
    correct_one = 1.0 - beta_one ** ADAM_STEP
    correct_two = 1.0 - beta_two ** ADAM_STEP
    weight_new = weight.astype(jnp.float32) - learn_rate * (first_new / correct_one) / (jnp.sqrt(second_new / correct_two) + adam_eps)
    return (weight_new.astype(jnp.bfloat16), first_new.astype(jnp.bfloat16), second_new.astype(jnp.bfloat16))

def group_sum(left, right):
    left_groups = left.reshape(N_DP, -1, left.shape[1]).astype(jnp.float32)
    right_groups = right.reshape(N_DP, -1, right.shape[1]).astype(jnp.float32)
    parts = jnp.einsum('gra,grb->gab', left_groups, right_groups, precision=lax.Precision.HIGHEST)
    rounded = lax.optimization_barrier(parts.astype(jnp.bfloat16))
    return lax.optimization_barrier(jnp.sum(rounded.astype(jnp.float32), axis=0))

def reference(tokens, routes, gates, cotangent, swap_flag, w_up, w_down, m_up, v_up, m_down, v_down):
    blocks = N_DP * N_EXPERT
    pair_block = TOK_DEV * TOP
    per_expert = blocks * CAP
    block_routes = routes.reshape(blocks, pair_block)
    one_hot = (block_routes[:, :, None] == jnp.arange(EXPERTS, dtype=jnp.int32)[None, None, :]).astype(jnp.int32)
    position = lax.optimization_barrier(jnp.sum(jnp.cumsum(one_hot, axis=1) * one_hot, axis=2)) - 1
    block_ids = jnp.arange(blocks, dtype=jnp.int32)[:, None]
    slot_index = (block_routes * per_expert + block_ids * CAP + position).reshape(-1).astype(jnp.int32)
    source = jnp.full((EXPERTS * per_expert,), -1, jnp.int32).at[slot_index].set(jnp.arange(blocks * pair_block, dtype=jnp.int32))
    flat_gates = gates.reshape(-1)

    def one_expert(inputs):
        up_weight, down_weight, up_first, up_second, down_first, down_second, expert_source = inputs
        is_live = expert_source >= 0
        safe_source = jnp.maximum(expert_source, 0)
        token_ids = safe_source // TOP
        expert_rows = jnp.where(is_live[:, None], tokens[token_ids], jnp.zeros((), tokens.dtype))
        live_gates = jnp.where(is_live, flat_gates[safe_source], jnp.zeros((), flat_gates.dtype))
        up_act = jnp.dot(expert_rows, up_weight, preferred_element_type=jnp.float32)
        hidden = jax.nn.silu(up_act).astype(jnp.bfloat16)
        expert_out = jnp.dot(hidden, down_weight, preferred_element_type=jnp.float32).astype(jnp.bfloat16)
        grad_rows = (live_gates[:, None] * cotangent[token_ids].astype(jnp.float32)).astype(jnp.bfloat16)
        hidden_grad = lax.dot_general(grad_rows, down_weight, (((1,), (1,)), ((), ())), preferred_element_type=jnp.float32)
        up_grad = (hidden_grad * silu_slope(up_act)).astype(jnp.bfloat16)
        input_part = lax.dot_general(up_grad, up_weight, (((1,), (1,)), ((), ())), preferred_element_type=jnp.float32).astype(jnp.bfloat16)
        up_gradient = group_sum(expert_rows, up_grad)
        down_gradient = group_sum(hidden, grad_rows)
        up_new = adam_update(up_weight, up_first, up_second, up_gradient)
        down_new = adam_update(down_weight, down_first, down_second, down_gradient)
        return (expert_out, input_part, up_new[0], down_new[0], up_new[1], up_new[2], down_new[1], down_new[2])
    results = lax.map(one_expert, (w_up, w_down, m_up, v_up, m_down, v_down, source.reshape(EXPERTS, per_expert)))
    flat_out = results[0].reshape(EXPERTS * per_expert, D)
    flat_input = results[1].reshape(EXPERTS * per_expert, D)
    picked = flat_out[slot_index].reshape(TOKENS, TOP, D)
    mixed = jnp.einsum('tk,tkd->td', gates.astype(jnp.float32), picked.astype(jnp.float32), precision=lax.Precision.HIGHEST).astype(jnp.bfloat16)
    picked_grad = flat_input[slot_index].reshape(TOKENS, TOP, D)
    input_grad = lax.optimization_barrier(jnp.sum(picked_grad.astype(jnp.float32), axis=1)).astype(jnp.bfloat16)
    placement = jnp.bitwise_xor(jnp.arange(EXPERTS, dtype=jnp.int32), swap_flag)
    return (mixed, input_grad, results[2][placement], results[3][placement], results[4][placement], results[5][placement], results[6][placement], results[7][placement])
```

```python
import jax
import jax.numpy as jnp
from jax import lax
from jax.sharding import PartitionSpec as P

ADAM_STEP = 10


beta_one = 0.9
beta_two = 0.95
learn_rate = 0.001
adam_eps = 1e-08


def partner(value, axis, distance):
    mask = 2**distance
    pairs = [(source, source ^ mask) for source in range(lax.axis_size(axis))]
    return lax.ppermute(value, axis, pairs)


def silu_slope(value):
    sigma = jax.nn.sigmoid(value)
    return sigma * (1.0 + value * (1.0 - sigma))


def adam_update(weight, first_moment, second_moment, gradient):
    first_new = beta_one * first_moment.astype(jnp.float32) + (1.0 - beta_one) * gradient
    second_new = (
        beta_two * second_moment.astype(jnp.float32) + (1.0 - beta_two) * gradient * gradient
    )
    correct_one = 1.0 - beta_one**ADAM_STEP
    correct_two = 1.0 - beta_two**ADAM_STEP
    weight_new = weight.astype(jnp.float32) - learn_rate * (first_new / correct_one) / (
        jnp.sqrt(second_new / correct_two) + adam_eps
    )
    return (
        weight_new.astype(jnp.bfloat16),
        first_new.astype(jnp.bfloat16),
        second_new.astype(jnp.bfloat16),
    )


def contract_rows(left, right):
    return lax.dot_general(
        left, right, (((0,), (0,)), ((), ())), preferred_element_type=jnp.float32
    )


def contract_cols(left, right):
    return lax.dot_general(
        left, right, (((1,), (1,)), ((), ())), preferred_element_type=jnp.float32
    )


def stack_state(members):
    return jnp.stack([member.reshape(-1) for member in members])


def unstack_state(stacked, member_shapes):
    return tuple(
        (stacked[number].reshape(member_shape) for number, member_shape in enumerate(member_shapes))
    )


def body(tokens, routes, gates, cotangent, swap_flag, w_up, w_down, m_up, v_up, m_down, v_down):
    experts = lax.axis_size("expert")
    my_slot = lax.axis_index("expert")
    tok_count, model_width = tokens.shape
    chosen = routes.shape[1]
    pair_count = tok_count * chosen
    capacity = pair_count * 4 // (3 * experts)
    row_total = experts * capacity
    my_flag = swap_flag[my_slot]
    swapped = my_flag == 1
    w_up_in = partner(w_up, "expert", 0)
    w_down_in = partner(w_down, "expert", 0)
    up_moments = partner(jnp.concatenate([m_up, v_up], axis=0), "expert", 0)
    down_moments = partner(jnp.concatenate([m_down, v_down], axis=0), "expert", 0)
    w_up_use = jnp.where(swapped, w_up_in, w_up)
    w_down_use = jnp.where(swapped, w_down_in, w_down)
    m_up_use = jnp.where(swapped, up_moments[0:1], m_up)
    v_up_use = jnp.where(swapped, up_moments[1:2], v_up)
    m_down_use = jnp.where(swapped, down_moments[0:1], m_down)
    v_down_use = jnp.where(swapped, down_moments[1:2], v_down)
    flat_routes = routes.reshape(pair_count)
    dest_routes = jnp.bitwise_xor(flat_routes, swap_flag[flat_routes])
    one_hot = (dest_routes[:, None] == jnp.arange(experts, dtype=jnp.int32)[None, :]).astype(
        jnp.int32
    )
    position = jnp.sum(jnp.cumsum(one_hot, axis=0) * one_hot, axis=1) - 1
    slot_index = dest_routes * capacity + position
    source = (
        jnp.full((row_total,), -1, jnp.int32)
        .at[slot_index]
        .set(jnp.arange(pair_count, dtype=jnp.int32))
    )
    is_live = source >= 0
    safe_source = jnp.maximum(source, 0)
    token_ids = safe_source // chosen
    send_tokens = jnp.where(
        is_live[:, None], tokens[token_ids], jnp.zeros((), jnp.bfloat16)
    ).reshape(experts, capacity, model_width)
    live_gates = jnp.where(is_live, gates.reshape(pair_count)[safe_source], 0.0)
    send_grads = (
        (live_gates[:, None] * cotangent[token_ids].astype(jnp.float32))
        .astype(jnp.bfloat16)
        .reshape(experts, capacity, model_width)
    )
    up_full = lax.all_gather(w_up_use, "dp", axis=1, tiled=True)[0]
    down_full = lax.all_gather(w_down_use, "dp", axis=1, tiled=True)[0]
    got_both = lax.all_to_all(
        jnp.concatenate([send_tokens, send_grads], axis=1),
        "expert",
        split_axis=0,
        concat_axis=0,
        tiled=True,
    )
    expert_rows = got_both[:, :capacity].reshape(row_total, model_width)
    grad_rows = got_both[:, capacity:].reshape(row_total, model_width)
    up_act = jnp.dot(expert_rows, up_full, preferred_element_type=jnp.float32)
    hidden = jax.nn.silu(up_act).astype(jnp.bfloat16)
    expert_out = jnp.dot(hidden, down_full, preferred_element_type=jnp.float32).astype(jnp.bfloat16)
    returned = lax.all_to_all(
        expert_out.reshape(experts, capacity, model_width),
        "expert",
        split_axis=0,
        concat_axis=0,
        tiled=True,
    )
    picked = returned.reshape(row_total, model_width)[slot_index].reshape(
        tok_count, chosen, model_width
    )
    mixed = jnp.sum(gates[:, :, None] * picked.astype(jnp.float32), axis=1).astype(jnp.bfloat16)
    hidden_grad = contract_cols(grad_rows, down_full)
    up_grad = (hidden_grad * silu_slope(up_act)).astype(jnp.bfloat16)
    input_part = contract_cols(up_grad, up_full).astype(jnp.bfloat16)
    back_grads = lax.all_to_all(
        input_part.reshape(experts, capacity, model_width),
        "expert",
        split_axis=0,
        concat_axis=0,
        tiled=True,
    )
    picked_grad = back_grads.reshape(row_total, model_width)[slot_index].reshape(
        tok_count, chosen, model_width
    )
    input_grad = jnp.sum(picked_grad.astype(jnp.float32), axis=1).astype(jnp.bfloat16)
    up_gradient = lax.psum_scatter(
        contract_rows(expert_rows, up_grad).astype(jnp.bfloat16),
        "dp",
        scatter_dimension=0,
        tiled=True,
    ).astype(jnp.float32)
    down_gradient = lax.psum_scatter(
        contract_rows(hidden, grad_rows).astype(jnp.bfloat16),
        "dp",
        scatter_dimension=0,
        tiled=True,
    ).astype(jnp.float32)
    up_new = adam_update(w_up_use[0], m_up_use[0], v_up_use[0], up_gradient)
    down_new = adam_update(w_down_use[0], m_down_use[0], v_down_use[0], down_gradient)
    return (
        mixed,
        input_grad,
        up_new[0][None],
        down_new[0][None],
        up_new[1][None],
        up_new[2][None],
        down_new[1][None],
        down_new[2][None],
    )


def solution(mesh):
    return jax.shard_map(
        body,
        mesh=mesh,
        in_specs=(
            P(("dp", "expert"), None),
            P(("dp", "expert"), None),
            P(("dp", "expert"), None),
            P(("dp", "expert"), None),
            P(),
            P("expert", "dp", None),
            P("expert", "dp", None),
            P("expert", "dp", None),
            P("expert", "dp", None),
            P("expert", "dp", None),
            P("expert", "dp", None),
        ),
        out_specs=(
            P(("dp", "expert"), None),
            P(("dp", "expert"), None),
            P("expert", "dp", None),
            P("expert", "dp", None),
            P("expert", "dp", None),
            P("expert", "dp", None),
            P("expert", "dp", None),
            P("expert", "dp", None),
        ),
        check_vma=False,
    )
```

```python
import jax
import jax.numpy as jnp
from jax import lax
from jax.sharding import PartitionSpec as P

ADAM_STEP = 10


beta_one = 0.9
beta_two = 0.95
learn_rate = 0.001
adam_eps = 1e-08


def partner(value, axis, distance):
    mask = 2**distance
    pairs = [(source, source ^ mask) for source in range(lax.axis_size(axis))]
    return lax.ppermute(value, axis, pairs)


def silu_slope(value):
    sigma = jax.nn.sigmoid(value)
    return sigma * (1.0 + value * (1.0 - sigma))


def adam_update(weight, first_moment, second_moment, gradient):
    first_new = beta_one * first_moment.astype(jnp.float32) + (1.0 - beta_one) * gradient
    second_new = (
        beta_two * second_moment.astype(jnp.float32) + (1.0 - beta_two) * gradient * gradient
    )
    correct_one = 1.0 - beta_one**ADAM_STEP
    correct_two = 1.0 - beta_two**ADAM_STEP
    weight_new = weight.astype(jnp.float32) - learn_rate * (first_new / correct_one) / (
        jnp.sqrt(second_new / correct_two) + adam_eps
    )
    return (
        weight_new.astype(jnp.bfloat16),
        first_new.astype(jnp.bfloat16),
        second_new.astype(jnp.bfloat16),
    )


def contract_rows(left, right):
    return lax.dot_general(
        left, right, (((0,), (0,)), ((), ())), preferred_element_type=jnp.float32
    )


def contract_cols(left, right):
    return lax.dot_general(
        left, right, (((1,), (1,)), ((), ())), preferred_element_type=jnp.float32
    )


def stack_state(members):
    return jnp.stack([member.reshape(-1) for member in members])


def unstack_state(stacked, member_shapes):
    return tuple(
        (stacked[number].reshape(member_shape) for number, member_shape in enumerate(member_shapes))
    )


def body(tokens, routes, gates, cotangent, swap_flag, w_up, w_down, m_up, v_up, m_down, v_down):
    experts = lax.axis_size("expert")
    my_slot = lax.axis_index("expert")
    tok_count, model_width = tokens.shape
    chosen = routes.shape[1]
    pair_count = tok_count * chosen
    capacity = pair_count * 4 // (3 * experts)
    row_total = experts * capacity
    swapped = swap_flag[my_slot] == 1
    w_up_in = partner(w_up, "expert", 0)
    w_down_in = partner(w_down, "expert", 0)
    w_up_in, w_down_in, up_local, down_local = lax.optimization_barrier(
        (
            w_up_in,
            w_down_in,
            jnp.concatenate([m_up, v_up], axis=0),
            jnp.concatenate([m_down, v_down], axis=0),
        )
    )
    up_moments = partner(up_local, "expert", 0)
    down_moments = partner(down_local, "expert", 0)
    w_up_use = jnp.where(swapped, w_up_in, w_up)
    w_down_use = jnp.where(swapped, w_down_in, w_down)
    up_full = lax.all_gather(w_up_use, "dp", axis=1, tiled=True)[0]
    down_full = lax.all_gather(w_down_use, "dp", axis=1, tiled=True)[0]
    expert_ids = jnp.arange(experts, dtype=jnp.int32)
    route_hot = (routes.reshape(pair_count)[:, None] == expert_ids[None, :]).astype(jnp.int32)
    paired_hot = route_hot.reshape(pair_count, experts // 2, 2)[:, :, ::-1].reshape(
        pair_count, experts
    )
    dest_hot = jnp.where(swap_flag[None, :] == 1, paired_hot, route_hot)
    position = jnp.sum(jnp.cumsum(dest_hot, axis=0) * dest_hot, axis=1) - 1
    slot_index = jnp.sum(dest_hot * (expert_ids * capacity)[None, :], axis=1) + position
    pick = slot_index[:, None] == jnp.arange(row_total, dtype=jnp.int32)[None, :]
    pick_bf = pick.astype(jnp.bfloat16)
    gather_rows = jnp.sum(pick_bf.reshape(tok_count, chosen, row_total), axis=1).T
    live_gates = jnp.sum(
        jnp.where(pick, gates.reshape(pair_count)[:, None], 0.0), axis=0
    )
    send_tokens = jnp.dot(gather_rows, tokens, preferred_element_type=jnp.float32).astype(
        jnp.bfloat16
    )
    send_cot = jnp.dot(gather_rows, cotangent, preferred_element_type=jnp.float32)
    send_grads = (live_gates[:, None] * send_cot).astype(jnp.bfloat16)
    got_both = lax.all_to_all(
        jnp.concatenate(
            [
                send_tokens.reshape(experts, capacity, model_width),
                send_grads.reshape(experts, capacity, model_width),
            ],
            axis=1,
        ),
        "expert",
        split_axis=0,
        concat_axis=0,
        tiled=True,
    )
    expert_rows = got_both[:, :capacity].reshape(row_total, model_width)
    grad_rows = got_both[:, capacity:].reshape(row_total, model_width)
    up_act = jnp.dot(expert_rows, up_full, preferred_element_type=jnp.float32)
    hidden = jax.nn.silu(up_act).astype(jnp.bfloat16)
    down_full, hidden, up_moments, down_moments = lax.optimization_barrier(
        (down_full, hidden, up_moments, down_moments)
    )
    expert_out = jnp.dot(hidden, down_full, preferred_element_type=jnp.float32).astype(jnp.bfloat16)
    returned = lax.all_to_all(
        expert_out.reshape(experts, capacity, model_width),
        "expert",
        split_axis=0,
        concat_axis=0,
        tiled=True,
    )
    picked = jnp.dot(
        pick_bf, returned.reshape(row_total, model_width), preferred_element_type=jnp.float32
    ).reshape(tok_count, chosen, model_width)
    mixed = jnp.sum(gates[:, :, None] * picked, axis=1).astype(jnp.bfloat16)
    hidden_grad = contract_cols(grad_rows, down_full)
    up_grad = (hidden_grad * silu_slope(up_act)).astype(jnp.bfloat16)
    input_part = contract_cols(up_grad, up_full).astype(jnp.bfloat16)
    back_grads = lax.all_to_all(
        input_part.reshape(experts, capacity, model_width),
        "expert",
        split_axis=0,
        concat_axis=0,
        tiled=True,
    )
    picked_grad = jnp.dot(
        pick_bf, back_grads.reshape(row_total, model_width), preferred_element_type=jnp.float32
    ).reshape(tok_count, chosen, model_width)
    input_grad = jnp.sum(picked_grad, axis=1).astype(jnp.bfloat16)
    up_gradient = lax.psum_scatter(
        contract_rows(expert_rows, up_grad).astype(jnp.bfloat16),
        "dp",
        scatter_dimension=0,
        tiled=True,
    ).astype(jnp.float32)
    down_gradient = lax.psum_scatter(
        contract_rows(hidden, grad_rows).astype(jnp.bfloat16),
        "dp",
        scatter_dimension=0,
        tiled=True,
    ).astype(jnp.float32)
    m_up_use = jnp.where(swapped, up_moments[0:1], m_up)
    v_up_use = jnp.where(swapped, up_moments[1:2], v_up)
    m_down_use = jnp.where(swapped, down_moments[0:1], m_down)
    v_down_use = jnp.where(swapped, down_moments[1:2], v_down)
    up_new = adam_update(w_up_use[0], m_up_use[0], v_up_use[0], up_gradient)
    down_new = adam_update(w_down_use[0], m_down_use[0], v_down_use[0], down_gradient)
    return (
        mixed,
        input_grad,
        up_new[0][None],
        down_new[0][None],
        up_new[1][None],
        up_new[2][None],
        down_new[1][None],
        down_new[2][None],
    )


def solution(mesh):
    return jax.shard_map(
        body,
        mesh=mesh,
        in_specs=(
            P(("dp", "expert"), None),
            P(("dp", "expert"), None),
            P(("dp", "expert"), None),
            P(("dp", "expert"), None),
            P(),
            P("expert", "dp", None),
            P("expert", "dp", None),
            P("expert", "dp", None),
            P("expert", "dp", None),
            P("expert", "dp", None),
            P("expert", "dp", None),
        ),
        out_specs=(
            P(("dp", "expert"), None),
            P(("dp", "expert"), None),
            P("expert", "dp", None),
            P("expert", "dp", None),
            P("expert", "dp", None),
            P("expert", "dp", None),
            P("expert", "dp", None),
            P("expert", "dp", None),
        ),
        check_vma=False,
    )
```

```python
import jax
import jax.numpy as jnp
from jax import lax
from jax.sharding import PartitionSpec as P

ADAM_STEP = 10


beta_one = 0.9
beta_two = 0.95
learn_rate = 0.001
adam_eps = 1e-08


def partner(value, axis, distance):
    mask = 2**distance
    pairs = [(source, source ^ mask) for source in range(lax.axis_size(axis))]
    return lax.ppermute(value, axis, pairs)


def silu_slope(value):
    sigma = jax.nn.sigmoid(value)
    return sigma * (1.0 + value * (1.0 - sigma))


def adam_update(weight, first_moment, second_moment, gradient):
    first_new = beta_one * first_moment.astype(jnp.float32) + (1.0 - beta_one) * gradient
    second_new = (
        beta_two * second_moment.astype(jnp.float32) + (1.0 - beta_two) * gradient * gradient
    )
    correct_one = 1.0 - beta_one**ADAM_STEP
    correct_two = 1.0 - beta_two**ADAM_STEP
    weight_new = weight.astype(jnp.float32) - learn_rate * (first_new / correct_one) / (
        jnp.sqrt(second_new / correct_two) + adam_eps
    )
    return (
        weight_new.astype(jnp.bfloat16),
        first_new.astype(jnp.bfloat16),
        second_new.astype(jnp.bfloat16),
    )


def contract_rows(left, right):
    return lax.dot_general(
        left, right, (((0,), (0,)), ((), ())), preferred_element_type=jnp.float32
    )


def contract_cols(left, right):
    return lax.dot_general(
        left, right, (((1,), (1,)), ((), ())), preferred_element_type=jnp.float32
    )


def stack_state(members):
    return jnp.stack([member.reshape(-1) for member in members])


def unstack_state(stacked, member_shapes):
    return tuple(
        (stacked[number].reshape(member_shape) for number, member_shape in enumerate(member_shapes))
    )


def body(tokens, routes, gates, cotangent, swap_flag, w_up, w_down, m_up, v_up, m_down, v_down):
    experts = lax.axis_size("expert")
    my_slot = lax.axis_index("expert")
    tok_count, model_width = tokens.shape
    chosen = routes.shape[1]
    pair_count = tok_count * chosen
    capacity = pair_count * 4 // (3 * experts)
    row_total = experts * capacity
    swapped = swap_flag[my_slot] == 1
    expert_ids = jnp.arange(experts, dtype=jnp.int32)
    route_hot = (routes.reshape(pair_count)[:, None] == expert_ids[None, :]).astype(jnp.int32)
    paired_hot = route_hot.reshape(pair_count, experts // 2, 2)[:, :, ::-1].reshape(
        pair_count, experts
    )
    dest_hot = jnp.where(swap_flag[None, :] == 1, paired_hot, route_hot)
    position = jnp.sum(jnp.cumsum(dest_hot, axis=0) * dest_hot, axis=1) - 1
    dest = jnp.sum(dest_hot * expert_ids[None, :], axis=1)
    slot_index = dest * capacity + position
    pick = slot_index[:, None] == jnp.arange(row_total, dtype=jnp.int32)[None, :]
    pick_bf = pick.astype(jnp.bfloat16)
    send_row = (dest * (2 * capacity) + position).reshape(tok_count, chosen)
    row_ids = jnp.arange(2 * row_total, dtype=jnp.int32)
    token_pick = jnp.sum(
        (send_row[:, :, None] == row_ids[None, None, :]).astype(jnp.bfloat16), axis=1
    )
    grad_pick = jnp.sum(
        (send_row[:, :, None] + capacity == row_ids[None, None, :]).astype(jnp.bfloat16), axis=1
    )
    row_scale = jnp.sum(
        jnp.where(
            send_row[:, :, None] + capacity == row_ids[None, None, :], gates[:, :, None], 0.0
        ),
        axis=(0, 1),
    ) + jnp.sum(token_pick.astype(jnp.float32), axis=0)
    picked_rows = lax.dot_general(
        jnp.concatenate([token_pick, grad_pick], axis=0),
        jnp.concatenate([tokens, cotangent], axis=0),
        (((0,), (0,)), ((), ())),
        preferred_element_type=jnp.float32,
    )
    send_both = (row_scale[:, None] * picked_rows).astype(jnp.bfloat16)
    w_up, w_down, send_both = lax.optimization_barrier((w_up, w_down, send_both))
    w_up_in = partner(w_up, "expert", 0)
    w_down_in = partner(w_down, "expert", 0)
    got_both = lax.all_to_all(
        send_both.reshape(experts, 2 * capacity, model_width),
        "expert",
        split_axis=0,
        concat_axis=0,
        tiled=True,
    )
    w_up_in, w_down_in, up_local, down_local = lax.optimization_barrier(
        (
            w_up_in,
            w_down_in,
            jnp.concatenate([m_up, v_up], axis=0),
            jnp.concatenate([m_down, v_down], axis=0),
        )
    )
    up_moments = partner(up_local, "expert", 0)
    down_moments = partner(down_local, "expert", 0)
    w_up_use = jnp.where(swapped, w_up_in, w_up)
    w_down_use = jnp.where(swapped, w_down_in, w_down)
    up_full = lax.all_gather(w_up_use, "dp", axis=1, tiled=True)[0]
    down_full = lax.all_gather(w_down_use, "dp", axis=1, tiled=True)[0]
    expert_rows = got_both[:, :capacity].reshape(row_total, model_width)
    grad_rows = got_both[:, capacity:].reshape(row_total, model_width)
    up_act = jnp.dot(expert_rows, up_full, preferred_element_type=jnp.float32)
    hidden = jax.nn.silu(up_act).astype(jnp.bfloat16)
    down_full, hidden, up_moments = lax.optimization_barrier((down_full, hidden, up_moments))
    expert_out = jnp.dot(hidden, down_full, preferred_element_type=jnp.float32).astype(jnp.bfloat16)
    hidden_grad = contract_cols(grad_rows, down_full)
    up_grad = (hidden_grad * silu_slope(up_act)).astype(jnp.bfloat16)
    input_part = contract_cols(up_grad, up_full).astype(jnp.bfloat16)
    both_back = lax.all_to_all(
        jnp.concatenate(
            [
                expert_out.reshape(experts, capacity, model_width),
                input_part.reshape(experts, capacity, model_width),
            ],
            axis=1,
        ),
        "expert",
        split_axis=0,
        concat_axis=0,
        tiled=True,
    )
    both_back, down_moments = lax.optimization_barrier((both_back, down_moments))
    picked = jnp.dot(
        pick_bf,
        both_back[:, :capacity].reshape(row_total, model_width),
        preferred_element_type=jnp.float32,
    ).reshape(tok_count, chosen, model_width)
    mixed = jnp.sum(gates[:, :, None] * picked, axis=1).astype(jnp.bfloat16)
    picked_grad = jnp.dot(
        pick_bf,
        both_back[:, capacity:].reshape(row_total, model_width),
        preferred_element_type=jnp.float32,
    ).reshape(tok_count, chosen, model_width)
    input_grad = jnp.sum(picked_grad, axis=1).astype(jnp.bfloat16)
    up_gradient = lax.psum_scatter(
        contract_rows(expert_rows, up_grad).astype(jnp.bfloat16),
        "dp",
        scatter_dimension=0,
        tiled=True,
    ).astype(jnp.float32)
    down_gradient = lax.psum_scatter(
        contract_rows(hidden, grad_rows).astype(jnp.bfloat16),
        "dp",
        scatter_dimension=0,
        tiled=True,
    ).astype(jnp.float32)
    m_up_use = jnp.where(swapped, up_moments[0:1], m_up)
    v_up_use = jnp.where(swapped, up_moments[1:2], v_up)
    m_down_use = jnp.where(swapped, down_moments[0:1], m_down)
    v_down_use = jnp.where(swapped, down_moments[1:2], v_down)
    up_new = adam_update(w_up_use[0], m_up_use[0], v_up_use[0], up_gradient)
    down_new = adam_update(w_down_use[0], m_down_use[0], v_down_use[0], down_gradient)
    return (
        mixed,
        input_grad,
        up_new[0][None],
        down_new[0][None],
        up_new[1][None],
        up_new[2][None],
        down_new[1][None],
        down_new[2][None],
    )


def solution(mesh):
    return jax.shard_map(
        body,
        mesh=mesh,
        in_specs=(
            P(("dp", "expert"), None),
            P(("dp", "expert"), None),
            P(("dp", "expert"), None),
            P(("dp", "expert"), None),
            P(),
            P("expert", "dp", None),
            P("expert", "dp", None),
            P("expert", "dp", None),
            P("expert", "dp", None),
            P("expert", "dp", None),
            P("expert", "dp", None),
        ),
        out_specs=(
            P(("dp", "expert"), None),
            P(("dp", "expert"), None),
            P("expert", "dp", None),
            P("expert", "dp", None),
            P("expert", "dp", None),
            P("expert", "dp", None),
            P("expert", "dp", None),
            P("expert", "dp", None),
        ),
        check_vma=False,
    )
```

```python
import jax
import jax.numpy as jnp
from jax import lax
from jax.sharding import PartitionSpec as P

ADAM_STEP = 10


beta_one = 0.9
beta_two = 0.95
learn_rate = 0.001
adam_eps = 1e-08


def partner(value, axis, distance):
    mask = 2**distance
    pairs = [(source, source ^ mask) for source in range(lax.axis_size(axis))]
    return lax.ppermute(value, axis, pairs)


def silu_slope(value):
    sigma = jax.nn.sigmoid(value)
    return sigma * (1.0 + value * (1.0 - sigma))


def adam_update(weight, first_moment, second_moment, gradient):
    first_new = beta_one * first_moment.astype(jnp.float32) + (1.0 - beta_one) * gradient
    second_new = (
        beta_two * second_moment.astype(jnp.float32) + (1.0 - beta_two) * gradient * gradient
    )
    correct_one = 1.0 - beta_one**ADAM_STEP
    correct_two = 1.0 - beta_two**ADAM_STEP
    weight_new = weight.astype(jnp.float32) - learn_rate * (first_new / correct_one) / (
        jnp.sqrt(second_new / correct_two) + adam_eps
    )
    return (
        weight_new.astype(jnp.bfloat16),
        first_new.astype(jnp.bfloat16),
        second_new.astype(jnp.bfloat16),
    )


def contract_rows(left, right):
    return lax.dot_general(
        left, right, (((0,), (0,)), ((), ())), preferred_element_type=jnp.float32
    )


def contract_cols(left, right):
    return lax.dot_general(
        left, right, (((1,), (1,)), ((), ())), preferred_element_type=jnp.float32
    )


def stack_state(members):
    return jnp.stack([member.reshape(-1) for member in members])


def unstack_state(stacked, member_shapes):
    return tuple(
        (stacked[number].reshape(member_shape) for number, member_shape in enumerate(member_shapes))
    )


def body(tokens, routes, gates, cotangent, swap_flag, w_up, w_down, m_up, v_up, m_down, v_down):
    experts = lax.axis_size("expert")
    my_slot = lax.axis_index("expert")
    tok_count, model_width = tokens.shape
    chosen = routes.shape[1]
    pair_count = tok_count * chosen
    capacity = pair_count * 4 // (3 * experts)
    row_total = experts * capacity
    swapped = swap_flag[my_slot] == 1
    expert_ids = jnp.arange(experts, dtype=jnp.int32)
    route_hot = (routes.reshape(pair_count)[:, None] == expert_ids[None, :]).astype(jnp.int32)
    paired_hot = route_hot.reshape(pair_count, experts // 2, 2)[:, :, ::-1].reshape(
        pair_count, experts
    )
    dest_hot = jnp.where(swap_flag[None, :] == 1, paired_hot, route_hot)
    position = jnp.sum(jnp.cumsum(dest_hot, axis=0) * dest_hot, axis=1) - 1
    dest = jnp.sum(dest_hot * expert_ids[None, :], axis=1)
    send_row = (dest * (2 * capacity) + position).reshape(tok_count, chosen)
    row_ids = jnp.arange(2 * row_total, dtype=jnp.int32)
    token_pick = jnp.sum(
        (send_row[:, :, None] == row_ids[None, None, :]).astype(jnp.bfloat16), axis=1
    )
    grad_pick = jnp.sum(
        (send_row[:, :, None] + capacity == row_ids[None, None, :]).astype(jnp.bfloat16), axis=1
    )
    row_scale = jnp.sum(
        jnp.where(
            send_row[:, :, None] + capacity == row_ids[None, None, :], gates[:, :, None], 0.0
        ),
        axis=(0, 1),
    ) + jnp.sum(token_pick.astype(jnp.float32), axis=0)
    picked_rows = lax.dot_general(
        jnp.concatenate([token_pick, grad_pick], axis=0),
        jnp.concatenate([tokens, cotangent], axis=0),
        (((0,), (0,)), ((), ())),
        preferred_element_type=jnp.float32,
    )
    send_both = (row_scale[:, None] * picked_rows).astype(jnp.bfloat16)
    w_up, w_down, send_both = lax.optimization_barrier((w_up, w_down, send_both))
    w_up_in = partner(w_up, "expert", 0)
    w_down_in = partner(w_down, "expert", 0)
    got_both = lax.all_to_all(
        send_both.reshape(experts, 2 * capacity, model_width),
        "expert",
        split_axis=0,
        concat_axis=0,
        tiled=True,
    )
    w_up_in, w_down_in, up_local, down_local = lax.optimization_barrier(
        (
            w_up_in,
            w_down_in,
            jnp.concatenate([m_up, v_up], axis=0),
            jnp.concatenate([m_down, v_down], axis=0),
        )
    )
    up_moments = partner(up_local, "expert", 0)
    w_up_use = jnp.where(swapped, w_up_in, w_up)
    w_down_use = jnp.where(swapped, w_down_in, w_down)
    up_full = lax.all_gather(w_up_use, "dp", axis=1, tiled=True)[0]
    down_full = lax.all_gather(w_down_use, "dp", axis=1, tiled=True)[0]
    expert_rows = got_both[:, :capacity].reshape(row_total, model_width)
    grad_rows = got_both[:, capacity:].reshape(row_total, model_width)
    up_act = jnp.dot(expert_rows, up_full, preferred_element_type=jnp.float32)
    hidden = jax.nn.silu(up_act).astype(jnp.bfloat16)
    down_full, hidden, up_moments, down_local = lax.optimization_barrier(
        (down_full, hidden, up_moments, down_local)
    )
    down_moments = partner(down_local, "expert", 0)
    expert_out = jnp.dot(hidden, down_full, preferred_element_type=jnp.float32).astype(jnp.bfloat16)
    hidden_grad = contract_cols(grad_rows, down_full)
    up_grad = (hidden_grad * silu_slope(up_act)).astype(jnp.bfloat16)
    input_part = contract_cols(up_grad, up_full).astype(jnp.bfloat16)
    input_part, down_moments = lax.optimization_barrier((input_part, down_moments))
    both_back = lax.all_to_all(
        jnp.concatenate(
            [
                expert_out.reshape(experts, capacity, model_width),
                input_part.reshape(experts, capacity, model_width),
            ],
            axis=1,
        ),
        "expert",
        split_axis=0,
        concat_axis=0,
        tiled=True,
    )
    back_rows = both_back.reshape(2 * row_total, model_width)
    picked = jnp.dot(
        (send_row.reshape(pair_count)[:, None] == row_ids[None, :]).astype(jnp.bfloat16),
        back_rows,
        preferred_element_type=jnp.float32,
    ).reshape(tok_count, chosen, model_width)
    mixed = jnp.sum(gates[:, :, None] * picked, axis=1).astype(jnp.bfloat16)
    picked_grad = jnp.dot(
        (send_row.reshape(pair_count)[:, None] + capacity == row_ids[None, :]).astype(
            jnp.bfloat16
        ),
        back_rows,
        preferred_element_type=jnp.float32,
    ).reshape(tok_count, chosen, model_width)
    input_grad = jnp.sum(picked_grad, axis=1).astype(jnp.bfloat16)
    up_gradient = lax.psum_scatter(
        contract_rows(expert_rows, up_grad).astype(jnp.bfloat16),
        "dp",
        scatter_dimension=0,
        tiled=True,
    ).astype(jnp.float32)
    down_gradient = lax.psum_scatter(
        contract_rows(hidden, grad_rows).astype(jnp.bfloat16),
        "dp",
        scatter_dimension=0,
        tiled=True,
    ).astype(jnp.float32)
    m_up_use = jnp.where(swapped, up_moments[0:1], m_up)
    v_up_use = jnp.where(swapped, up_moments[1:2], v_up)
    m_down_use = jnp.where(swapped, down_moments[0:1], m_down)
    v_down_use = jnp.where(swapped, down_moments[1:2], v_down)
    up_new = adam_update(w_up_use[0], m_up_use[0], v_up_use[0], up_gradient)
    down_new = adam_update(w_down_use[0], m_down_use[0], v_down_use[0], down_gradient)
    return (
        mixed,
        input_grad,
        up_new[0][None],
        down_new[0][None],
        up_new[1][None],
        up_new[2][None],
        down_new[1][None],
        down_new[2][None],
    )


def solution(mesh):
    return jax.shard_map(
        body,
        mesh=mesh,
        in_specs=(
            P(("dp", "expert"), None),
            P(("dp", "expert"), None),
            P(("dp", "expert"), None),
            P(("dp", "expert"), None),
            P(),
            P("expert", "dp", None),
            P("expert", "dp", None),
            P("expert", "dp", None),
            P("expert", "dp", None),
            P("expert", "dp", None),
            P("expert", "dp", None),
        ),
        out_specs=(
            P(("dp", "expert"), None),
            P(("dp", "expert"), None),
            P("expert", "dp", None),
            P("expert", "dp", None),
            P("expert", "dp", None),
            P("expert", "dp", None),
            P("expert", "dp", None),
            P("expert", "dp", None),
        ),
        check_vma=False,
    )
```

```python
import jax
import jax.numpy as jnp
from jax import lax
from jax.sharding import PartitionSpec as P

ADAM_STEP = 10


beta_one = 0.9
beta_two = 0.95
learn_rate = 0.001
adam_eps = 1e-08


def partner(value, axis, distance):
    mask = 2**distance
    pairs = [(source, source ^ mask) for source in range(lax.axis_size(axis))]
    return lax.ppermute(value, axis, pairs)


def silu_slope(value):
    sigma = jax.nn.sigmoid(value)
    return sigma * (1.0 + value * (1.0 - sigma))


def adam_update(weight, first_moment, second_moment, gradient):
    first_new = beta_one * first_moment.astype(jnp.float32) + (1.0 - beta_one) * gradient
    second_new = (
        beta_two * second_moment.astype(jnp.float32) + (1.0 - beta_two) * gradient * gradient
    )
    correct_one = 1.0 - beta_one**ADAM_STEP
    correct_two = 1.0 - beta_two**ADAM_STEP
    weight_new = weight.astype(jnp.float32) - learn_rate * (first_new / correct_one) / (
        jnp.sqrt(second_new / correct_two) + adam_eps
    )
    return (
        weight_new.astype(jnp.bfloat16),
        first_new.astype(jnp.bfloat16),
        second_new.astype(jnp.bfloat16),
    )


def contract_rows(left, right):
    return lax.dot_general(
        left, right, (((0,), (0,)), ((), ())), preferred_element_type=jnp.float32
    )


def contract_cols(left, right):
    return lax.dot_general(
        left, right, (((1,), (1,)), ((), ())), preferred_element_type=jnp.float32
    )


def stack_state(members):
    return jnp.stack([member.reshape(-1) for member in members])


def unstack_state(stacked, member_shapes):
    return tuple(
        (stacked[number].reshape(member_shape) for number, member_shape in enumerate(member_shapes))
    )


def body(tokens, routes, gates, cotangent, swap_flag, w_up, w_down, m_up, v_up, m_down, v_down):
    experts = lax.axis_size("expert")
    my_slot = lax.axis_index("expert")
    tok_count, model_width = tokens.shape
    chosen = routes.shape[1]
    pair_count = tok_count * chosen
    capacity = pair_count * 4 // (3 * experts)
    row_total = experts * capacity
    swapped = swap_flag[my_slot] == 1
    expert_ids = jnp.arange(experts, dtype=jnp.int32)
    route_hot = (routes.reshape(pair_count)[:, None] == expert_ids[None, :]).astype(jnp.int32)
    paired_hot = route_hot.reshape(pair_count, experts // 2, 2)[:, :, ::-1].reshape(
        pair_count, experts
    )
    dest_hot = jnp.where(swap_flag[None, :] == 1, paired_hot, route_hot)
    position = jnp.sum(jnp.cumsum(dest_hot, axis=0) * dest_hot, axis=1) - 1
    dest = jnp.sum(dest_hot * expert_ids[None, :], axis=1)
    half = capacity // 2
    chunk_rows = experts * 2 * half
    send_row = (
        (position // half) * chunk_rows + dest * (2 * half) + position % half
    ).reshape(tok_count, chosen)
    row_ids = jnp.arange(2 * chunk_rows, dtype=jnp.int32)
    token_hit = send_row[:, :, None] == row_ids[None, None, :]
    grad_hit = send_row[:, :, None] + half == row_ids[None, None, :]
    token_pick = jnp.sum(token_hit.astype(jnp.bfloat16), axis=1)
    grad_pick = jnp.sum(grad_hit.astype(jnp.bfloat16), axis=1)
    row_scale = jnp.sum(jnp.where(grad_hit, gates[:, :, None], 0.0), axis=(0, 1)) + jnp.sum(
        token_pick.astype(jnp.float32), axis=0
    )
    picked_rows = lax.dot_general(
        jnp.concatenate([token_pick, grad_pick], axis=0),
        jnp.concatenate([tokens, cotangent], axis=0),
        (((0,), (0,)), ((), ())),
        preferred_element_type=jnp.float32,
    )
    send_all = (row_scale[:, None] * picked_rows).astype(jnp.bfloat16)
    w_up, w_down, send_all = lax.optimization_barrier((w_up, w_down, send_all))
    w_up_in = partner(w_up, "expert", 0)
    w_down_in = partner(w_down, "expert", 0)
    got = [
        lax.all_to_all(
            send_all[number * chunk_rows : (number + 1) * chunk_rows].reshape(
                experts, 2 * half, model_width
            ),
            "expert",
            split_axis=0,
            concat_axis=0,
            tiled=True,
        )
        for number in range(2)
    ]
    w_up_in, w_down_in, up_local, down_local = lax.optimization_barrier(
        (
            w_up_in,
            w_down_in,
            jnp.concatenate([m_up, v_up], axis=0),
            jnp.concatenate([m_down, v_down], axis=0),
        )
    )
    up_moments = partner(up_local, "expert", 0)
    w_up_use = jnp.where(swapped, w_up_in, w_up)
    w_down_use = jnp.where(swapped, w_down_in, w_down)
    up_full = lax.all_gather(w_up_use, "dp", axis=1, tiled=True)[0]
    down_full = lax.all_gather(w_down_use, "dp", axis=1, tiled=True)[0]
    part_rows = experts * half
    back = []
    up_part = None
    down_part = None
    for number in range(2):
        expert_rows = got[number][:, :half].reshape(part_rows, model_width)
        grad_rows = got[number][:, half:].reshape(part_rows, model_width)
        up_act = jnp.dot(expert_rows, up_full, preferred_element_type=jnp.float32)
        hidden = jax.nn.silu(up_act).astype(jnp.bfloat16)
        if number == 0:
            down_full, hidden, up_moments, down_local = lax.optimization_barrier(
                (down_full, hidden, up_moments, down_local)
            )
            down_moments = partner(down_local, "expert", 0)
        expert_out = jnp.dot(hidden, down_full, preferred_element_type=jnp.float32).astype(
            jnp.bfloat16
        )
        hidden_grad = contract_cols(grad_rows, down_full)
        up_grad = (hidden_grad * silu_slope(up_act)).astype(jnp.bfloat16)
        input_part = contract_cols(up_grad, up_full).astype(jnp.bfloat16)
        if number == 1:
            input_part, down_moments = lax.optimization_barrier((input_part, down_moments))
        back.append(
            lax.all_to_all(
                jnp.concatenate(
                    [
                        expert_out.reshape(experts, half, model_width),
                        input_part.reshape(experts, half, model_width),
                    ],
                    axis=1,
                ),
                "expert",
                split_axis=0,
                concat_axis=0,
                tiled=True,
            ).reshape(chunk_rows, model_width)
        )
        up_term = contract_rows(expert_rows, up_grad)
        down_term = contract_rows(hidden, grad_rows)
        up_part = up_term if up_part is None else up_part + up_term
        down_part = down_term if down_part is None else down_part + down_term
    flat_row = send_row.reshape(pair_count)[:, None]
    picked = sum(
        jnp.dot(
            (flat_row == row_ids[None, number * chunk_rows : (number + 1) * chunk_rows]).astype(
                jnp.bfloat16
            ),
            back[number],
            preferred_element_type=jnp.float32,
        )
        for number in range(2)
    ).reshape(tok_count, chosen, model_width)
    mixed = jnp.sum(gates[:, :, None] * picked, axis=1).astype(jnp.bfloat16)
    picked_grad = sum(
        jnp.dot(
            (
                flat_row + half == row_ids[None, number * chunk_rows : (number + 1) * chunk_rows]
            ).astype(jnp.bfloat16),
            back[number],
            preferred_element_type=jnp.float32,
        )
        for number in range(2)
    ).reshape(tok_count, chosen, model_width)
    input_grad = jnp.sum(picked_grad, axis=1).astype(jnp.bfloat16)
    up_gradient = lax.psum_scatter(
        up_part.astype(jnp.bfloat16), "dp", scatter_dimension=0, tiled=True
    ).astype(jnp.float32)
    down_gradient = lax.psum_scatter(
        down_part.astype(jnp.bfloat16), "dp", scatter_dimension=0, tiled=True
    ).astype(jnp.float32)
    m_up_use = jnp.where(swapped, up_moments[0:1], m_up)
    v_up_use = jnp.where(swapped, up_moments[1:2], v_up)
    m_down_use = jnp.where(swapped, down_moments[0:1], m_down)
    v_down_use = jnp.where(swapped, down_moments[1:2], v_down)
    up_new = adam_update(w_up_use[0], m_up_use[0], v_up_use[0], up_gradient)
    down_new = adam_update(w_down_use[0], m_down_use[0], v_down_use[0], down_gradient)
    return (
        mixed,
        input_grad,
        up_new[0][None],
        down_new[0][None],
        up_new[1][None],
        up_new[2][None],
        down_new[1][None],
        down_new[2][None],
    )


def solution(mesh):
    return jax.shard_map(
        body,
        mesh=mesh,
        in_specs=(
            P(("dp", "expert"), None),
            P(("dp", "expert"), None),
            P(("dp", "expert"), None),
            P(("dp", "expert"), None),
            P(),
            P("expert", "dp", None),
            P("expert", "dp", None),
            P("expert", "dp", None),
            P("expert", "dp", None),
            P("expert", "dp", None),
            P("expert", "dp", None),
        ),
        out_specs=(
            P(("dp", "expert"), None),
            P(("dp", "expert"), None),
            P("expert", "dp", None),
            P("expert", "dp", None),
            P("expert", "dp", None),
            P("expert", "dp", None),
            P("expert", "dp", None),
            P("expert", "dp", None),
        ),
        check_vma=False,
    )
```

```python
import jax
import jax.numpy as jnp
from jax import lax
from jax.sharding import PartitionSpec as P

ADAM_STEP = 10


beta_one = 0.9
beta_two = 0.95
learn_rate = 0.001
adam_eps = 1e-08


def partner(value, axis, distance):
    mask = 2**distance
    pairs = [(source, source ^ mask) for source in range(lax.axis_size(axis))]
    return lax.ppermute(value, axis, pairs)


def silu_slope(value):
    sigma = jax.nn.sigmoid(value)
    return sigma * (1.0 + value * (1.0 - sigma))


def adam_update(weight, first_moment, second_moment, gradient):
    first_new = beta_one * first_moment.astype(jnp.float32) + (1.0 - beta_one) * gradient
    second_new = (
        beta_two * second_moment.astype(jnp.float32) + (1.0 - beta_two) * gradient * gradient
    )
    correct_one = 1.0 - beta_one**ADAM_STEP
    correct_two = 1.0 - beta_two**ADAM_STEP
    weight_new = weight.astype(jnp.float32) - learn_rate * (first_new / correct_one) / (
        jnp.sqrt(second_new / correct_two) + adam_eps
    )
    return (
        weight_new.astype(jnp.bfloat16),
        first_new.astype(jnp.bfloat16),
        second_new.astype(jnp.bfloat16),
    )


def contract_rows(left, right):
    return lax.dot_general(
        left, right, (((0,), (0,)), ((), ())), preferred_element_type=jnp.float32
    )


def contract_cols(left, right):
    return lax.dot_general(
        left, right, (((1,), (1,)), ((), ())), preferred_element_type=jnp.float32
    )


def stack_state(members):
    return jnp.stack([member.reshape(-1) for member in members])


def unstack_state(stacked, member_shapes):
    return tuple(
        (stacked[number].reshape(member_shape) for number, member_shape in enumerate(member_shapes))
    )


def body(tokens, routes, gates, cotangent, swap_flag, w_up, w_down, m_up, v_up, m_down, v_down):
    experts = lax.axis_size("expert")
    my_slot = lax.axis_index("expert")
    tok_count, model_width = tokens.shape
    chosen = routes.shape[1]
    pair_count = tok_count * chosen
    capacity = pair_count * 4 // (3 * experts)
    row_total = experts * capacity
    swapped = swap_flag[my_slot] == 1
    expert_ids = jnp.arange(experts, dtype=jnp.int32)
    route_hot = (routes.reshape(pair_count)[:, None] == expert_ids[None, :]).astype(jnp.int32)
    paired_hot = route_hot.reshape(pair_count, experts // 2, 2)[:, :, ::-1].reshape(
        pair_count, experts
    )
    dest_hot = jnp.where(swap_flag[None, :] == 1, paired_hot, route_hot)
    position = jnp.sum(jnp.cumsum(dest_hot, axis=0) * dest_hot, axis=1) - 1
    dest = jnp.sum(dest_hot * expert_ids[None, :], axis=1)
    send_row = (dest * (2 * capacity) + position).reshape(tok_count, chosen)
    row_ids = jnp.arange(2 * row_total, dtype=jnp.int32)
    token_pick = jnp.sum(
        (send_row[:, :, None] == row_ids[None, None, :]).astype(jnp.bfloat16), axis=1
    )
    grad_pick = jnp.sum(
        (send_row[:, :, None] + capacity == row_ids[None, None, :]).astype(jnp.bfloat16), axis=1
    )
    row_scale = jnp.sum(
        jnp.where(
            send_row[:, :, None] + capacity == row_ids[None, None, :], gates[:, :, None], 0.0
        ),
        axis=(0, 1),
    ) + jnp.sum(token_pick.astype(jnp.float32), axis=0)
    picked_rows = lax.dot_general(
        jnp.concatenate([token_pick, grad_pick], axis=0),
        jnp.concatenate([tokens, cotangent], axis=0),
        (((0,), (0,)), ((), ())),
        preferred_element_type=jnp.float32,
    )
    send_both = (row_scale[:, None] * picked_rows).astype(jnp.bfloat16)
    w_up_in = partner(w_up, "expert", 0)
    w_down_in = partner(w_down, "expert", 0)
    w_up_in, w_down_in, send_both, up_local, down_local = lax.optimization_barrier(
        (
            w_up_in,
            w_down_in,
            send_both,
            jnp.concatenate([m_up, v_up], axis=0),
            jnp.concatenate([m_down, v_down], axis=0),
        )
    )
    got_both = lax.all_to_all(
        send_both.reshape(experts, 2 * capacity, model_width),
        "expert",
        split_axis=0,
        concat_axis=0,
        tiled=True,
    )
    up_moments = partner(up_local, "expert", 0)
    w_up_use = jnp.where(swapped, w_up_in, w_up)
    w_down_use = jnp.where(swapped, w_down_in, w_down)
    up_full = lax.all_gather(w_up_use, "dp", axis=1, tiled=True)[0]
    down_full = lax.all_gather(w_down_use, "dp", axis=1, tiled=True)[0]
    expert_rows = got_both[:, :capacity].reshape(row_total, model_width)
    grad_rows = got_both[:, capacity:].reshape(row_total, model_width)
    up_act = jnp.dot(expert_rows, up_full, preferred_element_type=jnp.float32)
    hidden = jax.nn.silu(up_act).astype(jnp.bfloat16)
    down_full, hidden, up_moments, down_local = lax.optimization_barrier(
        (down_full, hidden, up_moments, down_local)
    )
    down_moments = partner(down_local, "expert", 0)
    expert_out = jnp.dot(hidden, down_full, preferred_element_type=jnp.float32).astype(jnp.bfloat16)
    hidden_grad = contract_cols(grad_rows, down_full)
    up_grad = (hidden_grad * silu_slope(up_act)).astype(jnp.bfloat16)
    input_part = contract_cols(up_grad, up_full).astype(jnp.bfloat16)
    input_part, down_moments = lax.optimization_barrier((input_part, down_moments))
    both_back = lax.all_to_all(
        jnp.concatenate(
            [
                expert_out.reshape(experts, capacity, model_width),
                input_part.reshape(experts, capacity, model_width),
            ],
            axis=1,
        ),
        "expert",
        split_axis=0,
        concat_axis=0,
        tiled=True,
    )
    back_rows = both_back.reshape(2 * row_total, model_width)
    picked = jnp.dot(
        (send_row.reshape(pair_count)[:, None] == row_ids[None, :]).astype(jnp.bfloat16),
        back_rows,
        preferred_element_type=jnp.float32,
    ).reshape(tok_count, chosen, model_width)
    mixed = jnp.sum(gates[:, :, None] * picked, axis=1).astype(jnp.bfloat16)
    picked_grad = jnp.dot(
        (send_row.reshape(pair_count)[:, None] + capacity == row_ids[None, :]).astype(
            jnp.bfloat16
        ),
        back_rows,
        preferred_element_type=jnp.float32,
    ).reshape(tok_count, chosen, model_width)
    input_grad = jnp.sum(picked_grad, axis=1).astype(jnp.bfloat16)
    up_gradient = lax.psum_scatter(
        contract_rows(expert_rows, up_grad).astype(jnp.bfloat16),
        "dp",
        scatter_dimension=0,
        tiled=True,
    ).astype(jnp.float32)
    down_gradient = lax.psum_scatter(
        contract_rows(hidden, grad_rows).astype(jnp.bfloat16),
        "dp",
        scatter_dimension=0,
        tiled=True,
    ).astype(jnp.float32)
    m_up_use = jnp.where(swapped, up_moments[0:1], m_up)
    v_up_use = jnp.where(swapped, up_moments[1:2], v_up)
    m_down_use = jnp.where(swapped, down_moments[0:1], m_down)
    v_down_use = jnp.where(swapped, down_moments[1:2], v_down)
    up_new = adam_update(w_up_use[0], m_up_use[0], v_up_use[0], up_gradient)
    down_new = adam_update(w_down_use[0], m_down_use[0], v_down_use[0], down_gradient)
    return (
        mixed,
        input_grad,
        up_new[0][None],
        down_new[0][None],
        up_new[1][None],
        up_new[2][None],
        down_new[1][None],
        down_new[2][None],
    )


def solution(mesh):
    return jax.shard_map(
        body,
        mesh=mesh,
        in_specs=(
            P(("dp", "expert"), None),
            P(("dp", "expert"), None),
            P(("dp", "expert"), None),
            P(("dp", "expert"), None),
            P(),
            P("expert", "dp", None),
            P("expert", "dp", None),
            P("expert", "dp", None),
            P("expert", "dp", None),
            P("expert", "dp", None),
            P("expert", "dp", None),
        ),
        out_specs=(
            P(("dp", "expert"), None),
            P(("dp", "expert"), None),
            P("expert", "dp", None),
            P("expert", "dp", None),
            P("expert", "dp", None),
            P("expert", "dp", None),
            P("expert", "dp", None),
            P("expert", "dp", None),
        ),
        check_vma=False,
    )
```

```python
import jax
import jax.numpy as jnp
from jax import lax
from jax.sharding import PartitionSpec as P

ADAM_STEP = 10


beta_one = 0.9
beta_two = 0.95
learn_rate = 0.001
adam_eps = 1e-08


def partner(value, axis, distance):
    mask = 2**distance
    pairs = [(source, source ^ mask) for source in range(lax.axis_size(axis))]
    return lax.ppermute(value, axis, pairs)


def silu_slope(value):
    sigma = jax.nn.sigmoid(value)
    return sigma * (1.0 + value * (1.0 - sigma))


def adam_update(weight, first_moment, second_moment, gradient):
    first_new = beta_one * first_moment.astype(jnp.float32) + (1.0 - beta_one) * gradient
    second_new = (
        beta_two * second_moment.astype(jnp.float32) + (1.0 - beta_two) * gradient * gradient
    )
    correct_one = 1.0 - beta_one**ADAM_STEP
    correct_two = 1.0 - beta_two**ADAM_STEP
    weight_new = weight.astype(jnp.float32) - learn_rate * (first_new / correct_one) / (
        jnp.sqrt(second_new / correct_two) + adam_eps
    )
    return (
        weight_new.astype(jnp.bfloat16),
        first_new.astype(jnp.bfloat16),
        second_new.astype(jnp.bfloat16),
    )


def contract_rows(left, right):
    return lax.dot_general(
        left, right, (((0,), (0,)), ((), ())), preferred_element_type=jnp.float32
    )


def contract_cols(left, right):
    return lax.dot_general(
        left, right, (((1,), (1,)), ((), ())), preferred_element_type=jnp.float32
    )


def stack_state(members):
    return jnp.stack([member.reshape(-1) for member in members])


def unstack_state(stacked, member_shapes):
    return tuple(
        (stacked[number].reshape(member_shape) for number, member_shape in enumerate(member_shapes))
    )


def body(tokens, routes, gates, cotangent, swap_flag, w_up, w_down, m_up, v_up, m_down, v_down):
    experts = lax.axis_size("expert")
    my_slot = lax.axis_index("expert")
    tok_count, model_width = tokens.shape
    chosen = routes.shape[1]
    pair_count = tok_count * chosen
    capacity = pair_count * 4 // (3 * experts)
    row_total = experts * capacity
    swapped = swap_flag[my_slot] == 1
    expert_ids = jnp.arange(experts, dtype=jnp.int32)
    route_hot = (routes.reshape(pair_count)[:, None] == expert_ids[None, :]).astype(jnp.int32)
    paired_hot = route_hot.reshape(pair_count, experts // 2, 2)[:, :, ::-1].reshape(
        pair_count, experts
    )
    dest_hot = jnp.where(swap_flag[None, :] == 1, paired_hot, route_hot)
    position = jnp.sum(jnp.cumsum(dest_hot, axis=0) * dest_hot, axis=1) - 1
    dest = jnp.sum(dest_hot * expert_ids[None, :], axis=1)
    send_row = (dest * (2 * capacity) + position).reshape(tok_count, chosen)
    row_ids = jnp.arange(2 * row_total, dtype=jnp.int32)
    token_pick = jnp.sum(
        (send_row[:, :, None] == row_ids[None, None, :]).astype(jnp.bfloat16), axis=1
    )
    grad_pick = jnp.sum(
        (send_row[:, :, None] + capacity == row_ids[None, None, :]).astype(jnp.bfloat16), axis=1
    )
    row_scale = jnp.sum(
        jnp.where(
            send_row[:, :, None] + capacity == row_ids[None, None, :], gates[:, :, None], 0.0
        ),
        axis=(0, 1),
    ) + jnp.sum(token_pick.astype(jnp.float32), axis=0)
    picked_rows = lax.dot_general(
        jnp.concatenate([token_pick, grad_pick], axis=0),
        jnp.concatenate([tokens, cotangent], axis=0),
        (((0,), (0,)), ((), ())),
        preferred_element_type=jnp.float32,
    )
    send_both = (row_scale[:, None] * picked_rows).astype(jnp.bfloat16)
    w_up_in = partner(w_up, "expert", 0)
    w_down_in = partner(w_down, "expert", 0)
    w_up_in, w_down_in, send_both, up_local, down_local = lax.optimization_barrier(
        (
            w_up_in,
            w_down_in,
            send_both,
            jnp.concatenate([m_up, v_up], axis=0),
            jnp.concatenate([m_down, v_down], axis=0),
        )
    )
    got_both = lax.all_to_all(
        send_both.reshape(experts, 2 * capacity, model_width),
        "expert",
        split_axis=0,
        concat_axis=0,
        tiled=True,
    )
    up_moments = partner(up_local, "expert", 0)
    w_up_use = jnp.where(swapped, w_up_in, w_up)
    w_down_use = jnp.where(swapped, w_down_in, w_down)
    up_full = lax.all_gather(w_up_use, "dp", axis=1, tiled=True)[0]
    down_full = lax.all_gather(w_down_use, "dp", axis=1, tiled=True)[0]
    slot_ids, buffer_ids = lax.optimization_barrier(
        (
            jnp.arange(row_total, dtype=jnp.int32),
            jnp.arange(2 * row_total, dtype=jnp.int32),
        )
    )
    token_at = (slot_ids // capacity) * (2 * capacity) + slot_ids % capacity
    take_token = (token_at[:, None] == buffer_ids[None, :]).astype(jnp.bfloat16)
    take_grad = (token_at[:, None] + capacity == buffer_ids[None, :]).astype(jnp.bfloat16)
    got_rows = got_both.reshape(2 * row_total, model_width)
    expert_rows = jnp.dot(take_token, got_rows, preferred_element_type=jnp.float32).astype(
        jnp.bfloat16
    )
    grad_rows = jnp.dot(take_grad, got_rows, preferred_element_type=jnp.float32).astype(
        jnp.bfloat16
    )
    up_act = jnp.dot(expert_rows, up_full, preferred_element_type=jnp.float32)
    hidden = jax.nn.silu(up_act).astype(jnp.bfloat16)
    down_full, hidden, up_moments, down_local = lax.optimization_barrier(
        (down_full, hidden, up_moments, down_local)
    )
    down_moments = partner(down_local, "expert", 0)
    expert_out = jnp.dot(hidden, down_full, preferred_element_type=jnp.float32).astype(jnp.bfloat16)
    hidden_grad = contract_cols(grad_rows, down_full)
    up_grad = (hidden_grad * silu_slope(up_act)).astype(jnp.bfloat16)
    input_part = contract_cols(up_grad, up_full).astype(jnp.bfloat16)
    input_part, down_moments = lax.optimization_barrier((input_part, down_moments))
    both_back = lax.all_to_all(
        (contract_rows(take_token, expert_out) + contract_rows(take_grad, input_part))
        .astype(jnp.bfloat16)
        .reshape(experts, 2 * capacity, model_width),
        "expert",
        split_axis=0,
        concat_axis=0,
        tiled=True,
    )
    back_rows = both_back.reshape(2 * row_total, model_width)
    picked = jnp.dot(
        (send_row.reshape(pair_count)[:, None] == row_ids[None, :]).astype(jnp.bfloat16),
        back_rows,
        preferred_element_type=jnp.float32,
    ).reshape(tok_count, chosen, model_width)
    mixed = jnp.sum(gates[:, :, None] * picked, axis=1).astype(jnp.bfloat16)
    picked_grad = jnp.dot(
        (send_row.reshape(pair_count)[:, None] + capacity == row_ids[None, :]).astype(
            jnp.bfloat16
        ),
        back_rows,
        preferred_element_type=jnp.float32,
    ).reshape(tok_count, chosen, model_width)
    input_grad = jnp.sum(picked_grad, axis=1).astype(jnp.bfloat16)
    up_gradient = lax.psum_scatter(
        contract_rows(expert_rows, up_grad).astype(jnp.bfloat16),
        "dp",
        scatter_dimension=0,
        tiled=True,
    ).astype(jnp.float32)
    down_gradient = lax.psum_scatter(
        contract_rows(hidden, grad_rows).astype(jnp.bfloat16),
        "dp",
        scatter_dimension=0,
        tiled=True,
    ).astype(jnp.float32)
    m_up_use = jnp.where(swapped, up_moments[0:1], m_up)
    v_up_use = jnp.where(swapped, up_moments[1:2], v_up)
    m_down_use = jnp.where(swapped, down_moments[0:1], m_down)
    v_down_use = jnp.where(swapped, down_moments[1:2], v_down)
    up_new = adam_update(w_up_use[0], m_up_use[0], v_up_use[0], up_gradient)
    down_new = adam_update(w_down_use[0], m_down_use[0], v_down_use[0], down_gradient)
    return (
        mixed,
        input_grad,
        up_new[0][None],
        down_new[0][None],
        up_new[1][None],
        up_new[2][None],
        down_new[1][None],
        down_new[2][None],
    )


def solution(mesh):
    return jax.shard_map(
        body,
        mesh=mesh,
        in_specs=(
            P(("dp", "expert"), None),
            P(("dp", "expert"), None),
            P(("dp", "expert"), None),
            P(("dp", "expert"), None),
            P(),
            P("expert", "dp", None),
            P("expert", "dp", None),
            P("expert", "dp", None),
            P("expert", "dp", None),
            P("expert", "dp", None),
            P("expert", "dp", None),
        ),
        out_specs=(
            P(("dp", "expert"), None),
            P(("dp", "expert"), None),
            P("expert", "dp", None),
            P("expert", "dp", None),
            P("expert", "dp", None),
            P("expert", "dp", None),
            P("expert", "dp", None),
            P("expert", "dp", None),
        ),
        check_vma=False,
    )
```

```python
import jax
import jax.numpy as jnp
from jax import lax
from jax.sharding import PartitionSpec as P

ADAM_STEP = 10


beta_one = 0.9
beta_two = 0.95
learn_rate = 0.001
adam_eps = 1e-08


def partner(value, axis, distance):
    mask = 2**distance
    pairs = [(source, source ^ mask) for source in range(lax.axis_size(axis))]
    return lax.ppermute(value, axis, pairs)


def silu_slope(value):
    sigma = jax.nn.sigmoid(value)
    return sigma * (1.0 + value * (1.0 - sigma))


def adam_update(weight, first_moment, second_moment, gradient):
    first_new = beta_one * first_moment.astype(jnp.float32) + (1.0 - beta_one) * gradient
    second_new = (
        beta_two * second_moment.astype(jnp.float32) + (1.0 - beta_two) * gradient * gradient
    )
    correct_one = 1.0 - beta_one**ADAM_STEP
    correct_two = 1.0 - beta_two**ADAM_STEP
    weight_new = weight.astype(jnp.float32) - learn_rate * (first_new / correct_one) / (
        jnp.sqrt(second_new / correct_two) + adam_eps
    )
    return (
        weight_new.astype(jnp.bfloat16),
        first_new.astype(jnp.bfloat16),
        second_new.astype(jnp.bfloat16),
    )


def contract_rows(left, right):
    return lax.dot_general(
        left, right, (((0,), (0,)), ((), ())), preferred_element_type=jnp.float32
    )


def contract_cols(left, right):
    return lax.dot_general(
        left, right, (((1,), (1,)), ((), ())), preferred_element_type=jnp.float32
    )


def stack_state(members):
    return jnp.stack([member.reshape(-1) for member in members])


def unstack_state(stacked, member_shapes):
    return tuple(
        (stacked[number].reshape(member_shape) for number, member_shape in enumerate(member_shapes))
    )


def body(tokens, routes, gates, cotangent, swap_flag, w_up, w_down, m_up, v_up, m_down, v_down):
    experts = lax.axis_size("expert")
    my_slot = lax.axis_index("expert")
    tok_count, model_width = tokens.shape
    chosen = routes.shape[1]
    pair_count = tok_count * chosen
    capacity = pair_count * 4 // (3 * experts)
    row_total = experts * capacity
    swapped = swap_flag[my_slot] == 1
    expert_ids = jnp.arange(experts, dtype=jnp.int32)
    route_hot = (routes.reshape(pair_count)[:, None] == expert_ids[None, :]).astype(jnp.int32)
    paired_hot = route_hot.reshape(pair_count, experts // 2, 2)[:, :, ::-1].reshape(
        pair_count, experts
    )
    dest_hot = jnp.where(swap_flag[None, :] == 1, paired_hot, route_hot)
    position = jnp.sum(jnp.cumsum(dest_hot, axis=0) * dest_hot, axis=1) - 1
    dest = jnp.sum(dest_hot * expert_ids[None, :], axis=1)
    send_row = (dest * (2 * capacity) + position).reshape(tok_count, chosen)
    row_ids = jnp.arange(2 * row_total, dtype=jnp.int32)
    token_pick = jnp.sum(
        (send_row[:, :, None] == row_ids[None, None, :]).astype(jnp.bfloat16), axis=1
    )
    grad_pick = jnp.sum(
        (send_row[:, :, None] + capacity == row_ids[None, None, :]).astype(jnp.bfloat16), axis=1
    )
    row_scale = jnp.sum(
        jnp.where(
            send_row[:, :, None] + capacity == row_ids[None, None, :], gates[:, :, None], 0.0
        ),
        axis=(0, 1),
    ) + jnp.sum(token_pick.astype(jnp.float32), axis=0)
    picked_rows = lax.dot_general(
        jnp.concatenate([token_pick, grad_pick], axis=0),
        jnp.concatenate([tokens, cotangent], axis=0),
        (((0,), (0,)), ((), ())),
        preferred_element_type=jnp.float32,
    )
    send_both = (row_scale[:, None] * picked_rows).astype(jnp.bfloat16)
    w_up_in = partner(w_up, "expert", 0)
    w_down_in = partner(w_down, "expert", 0)
    w_up_in, w_down_in, send_both, up_local, down_local = lax.optimization_barrier(
        (
            w_up_in,
            w_down_in,
            send_both,
            jnp.concatenate([m_up, v_up], axis=0),
            jnp.concatenate([m_down, v_down], axis=0),
        )
    )
    got_both = lax.all_to_all(
        send_both.reshape(experts, 2 * capacity, model_width),
        "expert",
        split_axis=0,
        concat_axis=0,
        tiled=True,
    )
    up_moments = partner(up_local, "expert", 0)
    w_up_use = jnp.where(swapped, w_up_in, w_up)
    w_down_use = jnp.where(swapped, w_down_in, w_down)
    up_full = lax.all_gather(w_up_use, "dp", axis=1, tiled=True)[0]
    down_full = lax.all_gather(w_down_use, "dp", axis=1, tiled=True)[0]
    slot_ids, buffer_ids = lax.optimization_barrier(
        (
            jnp.arange(row_total, dtype=jnp.int32),
            jnp.arange(2 * row_total, dtype=jnp.int32),
        )
    )
    token_at = (slot_ids // capacity) * (2 * capacity) + slot_ids % capacity
    take_token = (token_at[:, None] == buffer_ids[None, :]).astype(jnp.bfloat16)
    take_grad = (token_at[:, None] + capacity == buffer_ids[None, :]).astype(jnp.bfloat16)
    got_rows = got_both.reshape(2 * row_total, model_width)
    expert_rows = jnp.dot(take_token, got_rows, preferred_element_type=jnp.float32).astype(
        jnp.bfloat16
    )
    grad_rows = jnp.dot(take_grad, got_rows, preferred_element_type=jnp.float32).astype(
        jnp.bfloat16
    )
    up_act = jnp.dot(expert_rows, up_full, preferred_element_type=jnp.float32)
    hidden = jax.nn.silu(up_act).astype(jnp.bfloat16)
    down_full, hidden, up_moments, down_local = lax.optimization_barrier(
        (down_full, hidden, up_moments, down_local)
    )
    down_moments = partner(down_local, "expert", 0)
    expert_out = jnp.dot(hidden, down_full, preferred_element_type=jnp.float32).astype(jnp.bfloat16)
    hidden_grad = contract_cols(grad_rows, down_full)
    up_grad = (hidden_grad * silu_slope(up_act)).astype(jnp.bfloat16)
    input_part = contract_cols(up_grad, up_full).astype(jnp.bfloat16)
    input_part, down_moments = lax.optimization_barrier((input_part, down_moments))
    both_back = lax.all_to_all(
        (contract_rows(take_token, expert_out) + contract_rows(take_grad, input_part))
        .astype(jnp.bfloat16)
        .reshape(experts, 2 * capacity, model_width),
        "expert",
        split_axis=0,
        concat_axis=0,
        tiled=True,
    )
    up_gradient = lax.psum_scatter(
        contract_rows(expert_rows, up_grad).astype(jnp.bfloat16),
        "dp",
        scatter_dimension=0,
        tiled=True,
    ).astype(jnp.float32)
    down_gradient = lax.psum_scatter(
        contract_rows(hidden, grad_rows).astype(jnp.bfloat16),
        "dp",
        scatter_dimension=0,
        tiled=True,
    ).astype(jnp.float32)
    m_up_use = jnp.where(swapped, up_moments[0:1], m_up)
    v_up_use = jnp.where(swapped, up_moments[1:2], v_up)
    m_down_use = jnp.where(swapped, down_moments[0:1], m_down)
    v_down_use = jnp.where(swapped, down_moments[1:2], v_down)
    up_new = adam_update(w_up_use[0], m_up_use[0], v_up_use[0], up_gradient)
    down_new = adam_update(w_down_use[0], m_down_use[0], v_down_use[0], down_gradient)
    both_back, up_new, down_new = lax.optimization_barrier((both_back, up_new, down_new))
    back_rows = both_back.reshape(2 * row_total, model_width)
    picked = jnp.dot(
        (send_row.reshape(pair_count)[:, None] == row_ids[None, :]).astype(jnp.bfloat16),
        back_rows,
        preferred_element_type=jnp.float32,
    ).reshape(tok_count, chosen, model_width)
    mixed = jnp.sum(gates[:, :, None] * picked, axis=1).astype(jnp.bfloat16)
    picked_grad = jnp.dot(
        (send_row.reshape(pair_count)[:, None] + capacity == row_ids[None, :]).astype(
            jnp.bfloat16
        ),
        back_rows,
        preferred_element_type=jnp.float32,
    ).reshape(tok_count, chosen, model_width)
    input_grad = jnp.sum(picked_grad, axis=1).astype(jnp.bfloat16)
    return (
        mixed,
        input_grad,
        up_new[0][None],
        down_new[0][None],
        up_new[1][None],
        up_new[2][None],
        down_new[1][None],
        down_new[2][None],
    )


def solution(mesh):
    return jax.shard_map(
        body,
        mesh=mesh,
        in_specs=(
            P(("dp", "expert"), None),
            P(("dp", "expert"), None),
            P(("dp", "expert"), None),
            P(("dp", "expert"), None),
            P(),
            P("expert", "dp", None),
            P("expert", "dp", None),
            P("expert", "dp", None),
            P("expert", "dp", None),
            P("expert", "dp", None),
            P("expert", "dp", None),
        ),
        out_specs=(
            P(("dp", "expert"), None),
            P(("dp", "expert"), None),
            P("expert", "dp", None),
            P("expert", "dp", None),
            P("expert", "dp", None),
            P("expert", "dp", None),
            P("expert", "dp", None),
            P("expert", "dp", None),
        ),
        check_vma=False,
    )
```

```python
import jax
import jax.numpy as jnp
from jax import lax
from jax.sharding import PartitionSpec as P

ADAM_STEP = 10


beta_one = 0.9
beta_two = 0.95
learn_rate = 0.001
adam_eps = 1e-08


def partner(value, axis, distance):
    mask = 2**distance
    pairs = [(source, source ^ mask) for source in range(lax.axis_size(axis))]
    return lax.ppermute(value, axis, pairs)


def silu_slope(value):
    sigma = jax.nn.sigmoid(value)
    return sigma * (1.0 + value * (1.0 - sigma))


def adam_update(weight, first_moment, second_moment, gradient):
    first_new = beta_one * first_moment.astype(jnp.float32) + (1.0 - beta_one) * gradient
    second_new = (
        beta_two * second_moment.astype(jnp.float32) + (1.0 - beta_two) * gradient * gradient
    )
    correct_one = 1.0 - beta_one**ADAM_STEP
    correct_two = 1.0 - beta_two**ADAM_STEP
    weight_new = weight.astype(jnp.float32) - learn_rate * (first_new / correct_one) / (
        jnp.sqrt(second_new / correct_two) + adam_eps
    )
    return (
        weight_new.astype(jnp.bfloat16),
        first_new.astype(jnp.bfloat16),
        second_new.astype(jnp.bfloat16),
    )


def contract_rows(left, right):
    return lax.dot_general(
        left, right, (((0,), (0,)), ((), ())), preferred_element_type=jnp.float32
    )


def contract_cols(left, right):
    return lax.dot_general(
        left, right, (((1,), (1,)), ((), ())), preferred_element_type=jnp.float32
    )


def stack_state(members):
    return jnp.stack([member.reshape(-1) for member in members])


def unstack_state(stacked, member_shapes):
    return tuple(
        (stacked[number].reshape(member_shape) for number, member_shape in enumerate(member_shapes))
    )


def body(tokens, routes, gates, cotangent, swap_flag, w_up, w_down, m_up, v_up, m_down, v_down):
    experts = lax.axis_size("expert")
    my_slot = lax.axis_index("expert")
    tok_count, model_width = tokens.shape
    chosen = routes.shape[1]
    pair_count = tok_count * chosen
    capacity = pair_count * 4 // (3 * experts)
    row_total = experts * capacity
    swapped = swap_flag[my_slot] == 1
    expert_ids = jnp.arange(experts, dtype=jnp.int32)
    route_hot = (routes.reshape(pair_count)[:, None] == expert_ids[None, :]).astype(jnp.int32)
    paired_hot = route_hot.reshape(pair_count, experts // 2, 2)[:, :, ::-1].reshape(
        pair_count, experts
    )
    dest_hot = jnp.where(swap_flag[None, :] == 1, paired_hot, route_hot)
    position = jnp.sum(jnp.cumsum(dest_hot, axis=0) * dest_hot, axis=1) - 1
    dest = jnp.sum(dest_hot * expert_ids[None, :], axis=1)
    send_row = (dest * (2 * capacity) + position).reshape(tok_count, chosen)
    row_ids = jnp.arange(2 * row_total, dtype=jnp.int32)
    token_pick = jnp.sum(
        (send_row[:, :, None] == row_ids[None, None, :]).astype(jnp.bfloat16), axis=1
    )
    grad_pick = jnp.sum(
        (send_row[:, :, None] + capacity == row_ids[None, None, :]).astype(jnp.bfloat16), axis=1
    )
    row_scale = jnp.sum(
        jnp.where(
            send_row[:, :, None] + capacity == row_ids[None, None, :], gates[:, :, None], 0.0
        ),
        axis=(0, 1),
    ) + jnp.sum(token_pick.astype(jnp.float32), axis=0)
    picked_rows = lax.dot_general(
        jnp.concatenate([token_pick, grad_pick], axis=0),
        jnp.concatenate([tokens, cotangent], axis=0),
        (((0,), (0,)), ((), ())),
        preferred_element_type=jnp.float32,
    )
    send_both = (row_scale[:, None] * picked_rows).astype(jnp.bfloat16)
    w_up_in = partner(w_up, "expert", 0)
    w_down_in = partner(w_down, "expert", 0)
    w_up_in, w_down_in, send_both, up_local, down_local = lax.optimization_barrier(
        (
            w_up_in,
            w_down_in,
            send_both,
            jnp.concatenate([m_up, v_up], axis=0),
            jnp.concatenate([m_down, v_down], axis=0),
        )
    )
    got_both = lax.all_to_all(
        send_both.reshape(experts, 2 * capacity, model_width),
        "expert",
        split_axis=0,
        concat_axis=0,
        tiled=True,
    )
    up_moments = partner(up_local, "expert", 0)
    w_up_use = jnp.where(swapped, w_up_in, w_up)
    w_down_use = jnp.where(swapped, w_down_in, w_down)
    up_full = lax.all_gather(w_up_use, "dp", axis=1, tiled=True)[0]
    down_full = lax.all_gather(w_down_use, "dp", axis=1, tiled=True)[0]
    slot_ids, buffer_ids = lax.optimization_barrier(
        (
            jnp.arange(row_total, dtype=jnp.int32),
            jnp.arange(2 * row_total, dtype=jnp.int32),
        )
    )
    token_at = (slot_ids // capacity) * (2 * capacity) + slot_ids % capacity
    take_token = (token_at[:, None] == buffer_ids[None, :]).astype(jnp.bfloat16)
    take_grad = (token_at[:, None] + capacity == buffer_ids[None, :]).astype(jnp.bfloat16)
    got_rows = got_both.reshape(2 * row_total, model_width)
    expert_rows = jnp.dot(take_token, got_rows, preferred_element_type=jnp.float32).astype(
        jnp.bfloat16
    )
    grad_rows = jnp.dot(take_grad, got_rows, preferred_element_type=jnp.float32).astype(
        jnp.bfloat16
    )
    up_act = jnp.dot(expert_rows, up_full, preferred_element_type=jnp.float32)
    hidden = jax.nn.silu(up_act).astype(jnp.bfloat16)
    down_full, hidden, up_moments, down_local = lax.optimization_barrier(
        (down_full, hidden, up_moments, down_local)
    )
    down_moments = partner(down_local, "expert", 0)
    expert_out = jnp.dot(hidden, down_full, preferred_element_type=jnp.float32).astype(jnp.bfloat16)
    hidden_grad = contract_cols(grad_rows, down_full)
    up_grad = (hidden_grad * silu_slope(up_act)).astype(jnp.bfloat16)
    input_part = contract_cols(up_grad, up_full).astype(jnp.bfloat16)
    input_part, down_moments = lax.optimization_barrier((input_part, down_moments))
    both_back = lax.all_to_all(
        (contract_rows(take_token, expert_out) + contract_rows(take_grad, input_part))
        .astype(jnp.bfloat16)
        .reshape(experts, 2 * capacity, model_width),
        "expert",
        split_axis=0,
        concat_axis=0,
        tiled=True,
    )
    up_gradient = lax.psum_scatter(
        contract_rows(expert_rows, up_grad).astype(jnp.bfloat16),
        "dp",
        scatter_dimension=0,
        tiled=True,
    ).astype(jnp.float32)
    down_gradient = lax.psum_scatter(
        contract_rows(hidden, grad_rows).astype(jnp.bfloat16),
        "dp",
        scatter_dimension=0,
        tiled=True,
    ).astype(jnp.float32)
    m_up_use = jnp.where(swapped, up_moments[0:1], m_up)
    v_up_use = jnp.where(swapped, up_moments[1:2], v_up)
    m_down_use = jnp.where(swapped, down_moments[0:1], m_down)
    v_down_use = jnp.where(swapped, down_moments[1:2], v_down)
    up_new = adam_update(w_up_use[0], m_up_use[0], v_up_use[0], up_gradient)
    down_new = adam_update(w_down_use[0], m_down_use[0], v_down_use[0], down_gradient)
    both_back, up_new, down_new = lax.optimization_barrier((both_back, up_new, down_new))
    back_rows = both_back.reshape(2 * row_total, model_width)
    out_hit = send_row[:, :, None] == row_ids[None, None, :]
    mixed = jnp.dot(
        jnp.sum(jnp.where(out_hit, gates[:, :, None], 0.0), axis=1),
        back_rows.astype(jnp.float32),
        precision=lax.Precision.HIGHEST,
        preferred_element_type=jnp.float32,
    ).astype(jnp.bfloat16)
    input_grad = jnp.dot(
        jnp.sum((send_row[:, :, None] + capacity == row_ids[None, None, :]).astype(
            jnp.bfloat16
        ), axis=1),
        back_rows,
        preferred_element_type=jnp.float32,
    ).astype(jnp.bfloat16)
    return (
        mixed,
        input_grad,
        up_new[0][None],
        down_new[0][None],
        up_new[1][None],
        up_new[2][None],
        down_new[1][None],
        down_new[2][None],
    )


def solution(mesh):
    return jax.shard_map(
        body,
        mesh=mesh,
        in_specs=(
            P(("dp", "expert"), None),
            P(("dp", "expert"), None),
            P(("dp", "expert"), None),
            P(("dp", "expert"), None),
            P(),
            P("expert", "dp", None),
            P("expert", "dp", None),
            P("expert", "dp", None),
            P("expert", "dp", None),
            P("expert", "dp", None),
            P("expert", "dp", None),
        ),
        out_specs=(
            P(("dp", "expert"), None),
            P(("dp", "expert"), None),
            P("expert", "dp", None),
            P("expert", "dp", None),
            P("expert", "dp", None),
            P("expert", "dp", None),
            P("expert", "dp", None),
            P("expert", "dp", None),
        ),
        check_vma=False,
    )
```

```python
import jax
import jax.numpy as jnp
from jax import lax
from jax.sharding import PartitionSpec as P

ADAM_STEP = 10


beta_one = 0.9
beta_two = 0.95
learn_rate = 0.001
adam_eps = 1e-08


def partner(value, axis, distance):
    mask = 2**distance
    pairs = [(source, source ^ mask) for source in range(lax.axis_size(axis))]
    return lax.ppermute(value, axis, pairs)


def silu_slope(value):
    sigma = jax.nn.sigmoid(value)
    return sigma * (1.0 + value * (1.0 - sigma))


def adam_update(weight, first_moment, second_moment, gradient):
    first_new = beta_one * first_moment.astype(jnp.float32) + (1.0 - beta_one) * gradient
    second_new = (
        beta_two * second_moment.astype(jnp.float32) + (1.0 - beta_two) * gradient * gradient
    )
    correct_one = 1.0 - beta_one**ADAM_STEP
    correct_two = 1.0 - beta_two**ADAM_STEP
    weight_new = weight.astype(jnp.float32) - learn_rate * (first_new / correct_one) / (
        jnp.sqrt(second_new / correct_two) + adam_eps
    )
    return (
        weight_new.astype(jnp.bfloat16),
        first_new.astype(jnp.bfloat16),
        second_new.astype(jnp.bfloat16),
    )


def contract_rows(left, right):
    return lax.dot_general(
        left, right, (((0,), (0,)), ((), ())), preferred_element_type=jnp.float32
    )


def contract_cols(left, right):
    return lax.dot_general(
        left, right, (((1,), (1,)), ((), ())), preferred_element_type=jnp.float32
    )


def stack_state(members):
    return jnp.stack([member.reshape(-1) for member in members])


def unstack_state(stacked, member_shapes):
    return tuple(
        (stacked[number].reshape(member_shape) for number, member_shape in enumerate(member_shapes))
    )


def body(tokens, routes, gates, cotangent, swap_flag, w_up, w_down, m_up, v_up, m_down, v_down):
    experts = lax.axis_size("expert")
    my_slot = lax.axis_index("expert")
    tok_count, model_width = tokens.shape
    chosen = routes.shape[1]
    pair_count = tok_count * chosen
    capacity = pair_count * 4 // (3 * experts)
    row_total = experts * capacity
    swapped = swap_flag[my_slot] == 1
    expert_ids = jnp.arange(experts, dtype=jnp.int32)
    route_hot = (routes.reshape(pair_count)[:, None] == expert_ids[None, :]).astype(jnp.int32)
    paired_hot = route_hot.reshape(pair_count, experts // 2, 2)[:, :, ::-1].reshape(
        pair_count, experts
    )
    dest_hot = jnp.where(swap_flag[None, :] == 1, paired_hot, route_hot)
    position = jnp.sum(jnp.cumsum(dest_hot, axis=0) * dest_hot, axis=1) - 1
    dest = jnp.sum(dest_hot * expert_ids[None, :], axis=1)
    send_row = (dest * (2 * capacity) + position).reshape(tok_count, chosen)
    row_ids = jnp.arange(2 * row_total, dtype=jnp.int32)
    token_pick = jnp.sum(
        (send_row[:, :, None] == row_ids[None, None, :]).astype(jnp.bfloat16), axis=1
    )
    grad_pick = jnp.sum(
        (send_row[:, :, None] + capacity == row_ids[None, None, :]).astype(jnp.bfloat16), axis=1
    )
    row_scale = jnp.sum(
        jnp.where(
            send_row[:, :, None] + capacity == row_ids[None, None, :], gates[:, :, None], 0.0
        ),
        axis=(0, 1),
    ) + jnp.sum(token_pick.astype(jnp.float32), axis=0)
    picked_rows = lax.dot_general(
        jnp.concatenate([token_pick, grad_pick], axis=0),
        jnp.concatenate([tokens, cotangent], axis=0),
        (((0,), (0,)), ((), ())),
        preferred_element_type=jnp.float32,
    )
    send_both = (row_scale[:, None] * picked_rows).astype(jnp.bfloat16)
    w_up_in = partner(w_up, "expert", 0)
    w_down_in = partner(w_down, "expert", 0)
    w_up_in, w_down_in, send_both, up_local, down_local = lax.optimization_barrier(
        (
            w_up_in,
            w_down_in,
            send_both,
            jnp.concatenate([m_up, v_up], axis=0),
            jnp.concatenate([m_down, v_down], axis=0),
        )
    )
    got_both = lax.all_to_all(
        send_both.reshape(experts, 2 * capacity, model_width),
        "expert",
        split_axis=0,
        concat_axis=0,
        tiled=True,
    )
    up_moments = partner(up_local, "expert", 0)
    w_up_use = jnp.where(swapped, w_up_in, w_up)
    w_down_use = jnp.where(swapped, w_down_in, w_down)
    up_full = lax.all_gather(w_up_use, "dp", axis=1, tiled=True)[0]
    down_full = lax.all_gather(w_down_use, "dp", axis=1, tiled=True)[0]
    slot_ids, buffer_ids = lax.optimization_barrier(
        (
            jnp.arange(row_total, dtype=jnp.int32),
            jnp.arange(2 * row_total, dtype=jnp.int32),
        )
    )
    token_at = (slot_ids // capacity) * (2 * capacity) + slot_ids % capacity
    take_token = (token_at[:, None] == buffer_ids[None, :]).astype(jnp.bfloat16)
    take_grad = (token_at[:, None] + capacity == buffer_ids[None, :]).astype(jnp.bfloat16)
    got_rows = got_both.reshape(2 * row_total, model_width)
    expert_rows = jnp.dot(take_token, got_rows, preferred_element_type=jnp.float32).astype(
        jnp.bfloat16
    )
    grad_rows = jnp.dot(take_grad, got_rows, preferred_element_type=jnp.float32).astype(
        jnp.bfloat16
    )
    up_act = jnp.dot(expert_rows, up_full, preferred_element_type=jnp.float32)
    hidden = jax.nn.silu(up_act).astype(jnp.bfloat16)
    down_full, hidden = lax.optimization_barrier((down_full, hidden))
    down_part = contract_rows(hidden, grad_rows).astype(jnp.bfloat16)
    down_part, up_moments, down_local = lax.optimization_barrier(
        (down_part, up_moments, down_local)
    )
    down_moments = partner(down_local, "expert", 0)
    expert_out = jnp.dot(hidden, down_full, preferred_element_type=jnp.float32).astype(jnp.bfloat16)
    hidden_grad = contract_cols(grad_rows, down_full)
    up_grad = (hidden_grad * silu_slope(up_act)).astype(jnp.bfloat16)
    input_part = contract_cols(up_grad, up_full).astype(jnp.bfloat16)
    input_part, down_moments = lax.optimization_barrier((input_part, down_moments))
    both_back = lax.all_to_all(
        (contract_rows(take_token, expert_out) + contract_rows(take_grad, input_part))
        .astype(jnp.bfloat16)
        .reshape(experts, 2 * capacity, model_width),
        "expert",
        split_axis=0,
        concat_axis=0,
        tiled=True,
    )
    up_gradient = lax.psum_scatter(
        contract_rows(expert_rows, up_grad).astype(jnp.bfloat16),
        "dp",
        scatter_dimension=0,
        tiled=True,
    ).astype(jnp.float32)
    down_gradient = lax.psum_scatter(
        down_part,
        "dp",
        scatter_dimension=0,
        tiled=True,
    ).astype(jnp.float32)
    m_up_use = jnp.where(swapped, up_moments[0:1], m_up)
    v_up_use = jnp.where(swapped, up_moments[1:2], v_up)
    m_down_use = jnp.where(swapped, down_moments[0:1], m_down)
    v_down_use = jnp.where(swapped, down_moments[1:2], v_down)
    up_new = adam_update(w_up_use[0], m_up_use[0], v_up_use[0], up_gradient)
    down_new = adam_update(w_down_use[0], m_down_use[0], v_down_use[0], down_gradient)
    both_back, up_new, down_new = lax.optimization_barrier((both_back, up_new, down_new))
    back_rows = both_back.reshape(2 * row_total, model_width)
    out_hit = send_row[:, :, None] == row_ids[None, None, :]
    mixed = jnp.dot(
        jnp.sum(jnp.where(out_hit, gates[:, :, None], 0.0), axis=1),
        back_rows.astype(jnp.float32),
        precision=lax.Precision.HIGHEST,
        preferred_element_type=jnp.float32,
    ).astype(jnp.bfloat16)
    input_grad = jnp.dot(
        jnp.sum((send_row[:, :, None] + capacity == row_ids[None, None, :]).astype(
            jnp.bfloat16
        ), axis=1),
        back_rows,
        preferred_element_type=jnp.float32,
    ).astype(jnp.bfloat16)
    return (
        mixed,
        input_grad,
        up_new[0][None],
        down_new[0][None],
        up_new[1][None],
        up_new[2][None],
        down_new[1][None],
        down_new[2][None],
    )


def solution(mesh):
    return jax.shard_map(
        body,
        mesh=mesh,
        in_specs=(
            P(("dp", "expert"), None),
            P(("dp", "expert"), None),
            P(("dp", "expert"), None),
            P(("dp", "expert"), None),
            P(),
            P("expert", "dp", None),
            P("expert", "dp", None),
            P("expert", "dp", None),
            P("expert", "dp", None),
            P("expert", "dp", None),
            P("expert", "dp", None),
        ),
        out_specs=(
            P(("dp", "expert"), None),
            P(("dp", "expert"), None),
            P("expert", "dp", None),
            P("expert", "dp", None),
            P("expert", "dp", None),
            P("expert", "dp", None),
            P("expert", "dp", None),
            P("expert", "dp", None),
        ),
        check_vma=False,
    )
```

```python
import jax
import jax.numpy as jnp
from jax import lax
from jax.sharding import PartitionSpec as P

ADAM_STEP = 10


beta_one = 0.9
beta_two = 0.95
learn_rate = 0.001
adam_eps = 1e-08


def partner(value, axis, distance):
    mask = 2**distance
    pairs = [(source, source ^ mask) for source in range(lax.axis_size(axis))]
    return lax.ppermute(value, axis, pairs)


def silu_slope(value):
    sigma = jax.nn.sigmoid(value)
    return sigma * (1.0 + value * (1.0 - sigma))


def adam_update(weight, first_moment, second_moment, gradient):
    first_new = beta_one * first_moment.astype(jnp.float32) + (1.0 - beta_one) * gradient
    second_new = (
        beta_two * second_moment.astype(jnp.float32) + (1.0 - beta_two) * gradient * gradient
    )
    correct_one = 1.0 - beta_one**ADAM_STEP
    correct_two = 1.0 - beta_two**ADAM_STEP
    weight_new = weight.astype(jnp.float32) - learn_rate * (first_new / correct_one) / (
        jnp.sqrt(second_new / correct_two) + adam_eps
    )
    return (
        weight_new.astype(jnp.bfloat16),
        first_new.astype(jnp.bfloat16),
        second_new.astype(jnp.bfloat16),
    )


def contract_rows(left, right):
    return lax.dot_general(
        left, right, (((0,), (0,)), ((), ())), preferred_element_type=jnp.float32
    )


def contract_cols(left, right):
    return lax.dot_general(
        left, right, (((1,), (1,)), ((), ())), preferred_element_type=jnp.float32
    )


def stack_state(members):
    return jnp.stack([member.reshape(-1) for member in members])


def unstack_state(stacked, member_shapes):
    return tuple(
        (stacked[number].reshape(member_shape) for number, member_shape in enumerate(member_shapes))
    )


def body(tokens, routes, gates, cotangent, swap_flag, w_up, w_down, m_up, v_up, m_down, v_down):
    experts = lax.axis_size("expert")
    my_slot = lax.axis_index("expert")
    tok_count, model_width = tokens.shape
    chosen = routes.shape[1]
    pair_count = tok_count * chosen
    capacity = pair_count * 4 // (3 * experts)
    row_total = experts * capacity
    swapped = swap_flag[my_slot] == 1
    expert_ids = jnp.arange(experts, dtype=jnp.int32)
    route_hot = (routes.reshape(pair_count)[:, None] == expert_ids[None, :]).astype(jnp.int32)
    paired_hot = route_hot.reshape(pair_count, experts // 2, 2)[:, :, ::-1].reshape(
        pair_count, experts
    )
    dest_hot = jnp.where(swap_flag[None, :] == 1, paired_hot, route_hot)
    position = jnp.sum(jnp.cumsum(dest_hot, axis=0) * dest_hot, axis=1) - 1
    dest = jnp.sum(dest_hot * expert_ids[None, :], axis=1)
    send_row = (dest * (2 * capacity) + position).reshape(tok_count, chosen)
    row_ids = jnp.arange(2 * row_total, dtype=jnp.int32)
    token_pick = jnp.sum(
        (send_row[:, :, None] == row_ids[None, None, :]).astype(jnp.bfloat16), axis=1
    )
    grad_pick = jnp.sum(
        (send_row[:, :, None] + capacity == row_ids[None, None, :]).astype(jnp.bfloat16), axis=1
    )
    row_scale = jnp.sum(
        jnp.where(
            send_row[:, :, None] + capacity == row_ids[None, None, :], gates[:, :, None], 0.0
        ),
        axis=(0, 1),
    ) + jnp.sum(token_pick.astype(jnp.float32), axis=0)
    picked_rows = lax.dot_general(
        jnp.concatenate([token_pick, grad_pick], axis=0),
        jnp.concatenate([tokens, cotangent], axis=0),
        (((0,), (0,)), ((), ())),
        preferred_element_type=jnp.float32,
    )
    send_both = (row_scale[:, None] * picked_rows).astype(jnp.bfloat16)
    w_up_in = partner(w_up, "expert", 0)
    w_down_in = partner(w_down, "expert", 0)
    w_up_in, w_down_in, send_both, up_local, down_local = lax.optimization_barrier(
        (
            w_up_in,
            w_down_in,
            send_both,
            jnp.concatenate([m_up, v_up], axis=0),
            jnp.concatenate([m_down, v_down], axis=0),
        )
    )
    got_both = lax.all_to_all(
        send_both.reshape(experts, 2 * capacity, model_width),
        "expert",
        split_axis=0,
        concat_axis=0,
        tiled=True,
    )
    up_moments = partner(up_local, "expert", 0)
    w_up_use = jnp.where(swapped, w_up_in, w_up)
    w_down_use = jnp.where(swapped, w_down_in, w_down)
    up_full = lax.all_gather(w_up_use, "dp", axis=1, tiled=True)[0]
    down_full = lax.all_gather(w_down_use, "dp", axis=1, tiled=True)[0]
    slot_ids, buffer_ids = lax.optimization_barrier(
        (
            jnp.arange(row_total, dtype=jnp.int32),
            jnp.arange(2 * row_total, dtype=jnp.int32),
        )
    )
    token_at = (slot_ids // capacity) * (2 * capacity) + slot_ids % capacity
    take_token = (token_at[:, None] == buffer_ids[None, :]).astype(jnp.bfloat16)
    take_grad = (token_at[:, None] + capacity == buffer_ids[None, :]).astype(jnp.bfloat16)
    got_rows = got_both.reshape(2 * row_total, model_width)
    expert_rows = jnp.dot(take_token, got_rows, preferred_element_type=jnp.float32).astype(
        jnp.bfloat16
    )
    grad_rows = jnp.dot(take_grad, got_rows, preferred_element_type=jnp.float32).astype(
        jnp.bfloat16
    )
    up_act = jnp.dot(expert_rows, up_full, preferred_element_type=jnp.float32)
    hidden = jax.nn.silu(up_act).astype(jnp.bfloat16)
    down_full, hidden = lax.optimization_barrier((down_full, hidden))
    down_part = contract_rows(hidden, grad_rows).astype(jnp.bfloat16)
    down_part, up_moments, down_local = lax.optimization_barrier(
        (down_part, up_moments, down_local)
    )
    down_moments = partner(down_local, "expert", 0)
    expert_out = jnp.dot(hidden, down_full, preferred_element_type=jnp.float32).astype(jnp.bfloat16)
    hidden_grad = contract_cols(grad_rows, down_full)
    up_grad = (hidden_grad * silu_slope(up_act)).astype(jnp.bfloat16)
    input_part = contract_cols(up_grad, up_full).astype(jnp.bfloat16)
    input_part, down_moments = lax.optimization_barrier((input_part, down_moments))
    both_back = lax.all_to_all(
        (contract_rows(take_token, expert_out) + contract_rows(take_grad, input_part))
        .astype(jnp.bfloat16)
        .reshape(experts, 2 * capacity, model_width),
        "expert",
        split_axis=0,
        concat_axis=0,
        tiled=True,
    )
    up_gradient = lax.psum_scatter(
        contract_rows(expert_rows, up_grad).astype(jnp.bfloat16),
        "dp",
        scatter_dimension=0,
        tiled=True,
    ).astype(jnp.float32)
    down_gradient = lax.psum_scatter(
        down_part,
        "dp",
        scatter_dimension=0,
        tiled=True,
    ).astype(jnp.float32)
    m_up_use = jnp.where(swapped, up_moments[0:1], m_up)
    v_up_use = jnp.where(swapped, up_moments[1:2], v_up)
    m_down_use = jnp.where(swapped, down_moments[0:1], m_down)
    v_down_use = jnp.where(swapped, down_moments[1:2], v_down)
    up_new = adam_update(w_up_use[0], m_up_use[0], v_up_use[0], up_gradient)
    down_new = adam_update(w_down_use[0], m_down_use[0], v_down_use[0], down_gradient)
    both_back, up_new, down_new = lax.optimization_barrier((both_back, up_new, down_new))
    back_rows = both_back.reshape(2 * row_total, model_width)
    out_hit = send_row[:, :, None] == row_ids[None, None, :]
    gate_rows = jnp.sum(jnp.where(out_hit, gates[:, :, None], 0.0), axis=1)
    gate_hi = gate_rows.astype(jnp.bfloat16)
    gate_rest = gate_rows - gate_hi.astype(jnp.float32)
    gate_mid = gate_rest.astype(jnp.bfloat16)
    gate_lo = (gate_rest - gate_mid.astype(jnp.float32)).astype(jnp.bfloat16)
    mixed = jnp.dot(
        jnp.concatenate([gate_hi, gate_mid, gate_lo], axis=1),
        jnp.concatenate([back_rows, back_rows, back_rows], axis=0),
        preferred_element_type=jnp.float32,
    ).astype(jnp.bfloat16)
    input_grad = jnp.dot(
        jnp.sum((send_row[:, :, None] + capacity == row_ids[None, None, :]).astype(
            jnp.bfloat16
        ), axis=1),
        back_rows,
        preferred_element_type=jnp.float32,
    ).astype(jnp.bfloat16)
    return (
        mixed,
        input_grad,
        up_new[0][None],
        down_new[0][None],
        up_new[1][None],
        up_new[2][None],
        down_new[1][None],
        down_new[2][None],
    )


def solution(mesh):
    return jax.shard_map(
        body,
        mesh=mesh,
        in_specs=(
            P(("dp", "expert"), None),
            P(("dp", "expert"), None),
            P(("dp", "expert"), None),
            P(("dp", "expert"), None),
            P(),
            P("expert", "dp", None),
            P("expert", "dp", None),
            P("expert", "dp", None),
            P("expert", "dp", None),
            P("expert", "dp", None),
            P("expert", "dp", None),
        ),
        out_specs=(
            P(("dp", "expert"), None),
            P(("dp", "expert"), None),
            P("expert", "dp", None),
            P("expert", "dp", None),
            P("expert", "dp", None),
            P("expert", "dp", None),
            P("expert", "dp", None),
            P("expert", "dp", None),
        ),
        check_vma=False,
    )
```

```python
import jax
import jax.numpy as jnp
from jax import lax
from jax.sharding import PartitionSpec as P

ADAM_STEP = 10


beta_one = 0.9
beta_two = 0.95
learn_rate = 0.001
adam_eps = 1e-08


def partner(value, axis, distance):
    mask = 2**distance
    pairs = [(source, source ^ mask) for source in range(lax.axis_size(axis))]
    return lax.ppermute(value, axis, pairs)


def silu_slope(value):
    sigma = jax.nn.sigmoid(value)
    return sigma * (1.0 + value * (1.0 - sigma))


def adam_update(weight, first_moment, second_moment, gradient):
    first_new = beta_one * first_moment.astype(jnp.float32) + (1.0 - beta_one) * gradient
    second_new = (
        beta_two * second_moment.astype(jnp.float32) + (1.0 - beta_two) * gradient * gradient
    )
    correct_one = 1.0 - beta_one**ADAM_STEP
    correct_two = 1.0 - beta_two**ADAM_STEP
    weight_new = weight.astype(jnp.float32) - learn_rate * (first_new / correct_one) / (
        jnp.sqrt(second_new / correct_two) + adam_eps
    )
    return (
        weight_new.astype(jnp.bfloat16),
        first_new.astype(jnp.bfloat16),
        second_new.astype(jnp.bfloat16),
    )


def contract_rows(left, right):
    return lax.dot_general(
        left, right, (((0,), (0,)), ((), ())), preferred_element_type=jnp.float32
    )


def contract_cols(left, right):
    return lax.dot_general(
        left, right, (((1,), (1,)), ((), ())), preferred_element_type=jnp.float32
    )


def stack_state(members):
    return jnp.stack([member.reshape(-1) for member in members])


def unstack_state(stacked, member_shapes):
    return tuple(
        (stacked[number].reshape(member_shape) for number, member_shape in enumerate(member_shapes))
    )


def body(tokens, routes, gates, cotangent, swap_flag, w_up, w_down, m_up, v_up, m_down, v_down):
    experts = lax.axis_size("expert")
    my_slot = lax.axis_index("expert")
    tok_count, model_width = tokens.shape
    chosen = routes.shape[1]
    pair_count = tok_count * chosen
    capacity = pair_count * 4 // (3 * experts)
    row_total = experts * capacity
    swapped = swap_flag[my_slot] == 1
    expert_ids = jnp.arange(experts, dtype=jnp.int32)
    route_hot = (routes.reshape(pair_count)[:, None] == expert_ids[None, :]).astype(jnp.int32)
    paired_hot = route_hot.reshape(pair_count, experts // 2, 2)[:, :, ::-1].reshape(
        pair_count, experts
    )
    dest_hot = jnp.where(swap_flag[None, :] == 1, paired_hot, route_hot)
    position = jnp.sum(jnp.cumsum(dest_hot, axis=0) * dest_hot, axis=1) - 1
    dest = jnp.sum(dest_hot * expert_ids[None, :], axis=1)
    send_row = (dest * (2 * capacity) + position).reshape(tok_count, chosen)
    row_ids = jnp.arange(2 * row_total, dtype=jnp.int32)
    token_pick = jnp.sum(
        (send_row[:, :, None] == row_ids[None, None, :]).astype(jnp.bfloat16), axis=1
    )
    grad_pick = jnp.sum(
        (send_row[:, :, None] + capacity == row_ids[None, None, :]).astype(jnp.bfloat16), axis=1
    )
    row_scale = jnp.sum(
        jnp.where(
            send_row[:, :, None] + capacity == row_ids[None, None, :], gates[:, :, None], 0.0
        ),
        axis=(0, 1),
    ) + jnp.sum(token_pick.astype(jnp.float32), axis=0)
    picked_rows = lax.dot_general(
        jnp.concatenate([token_pick, grad_pick], axis=0),
        jnp.concatenate([tokens, cotangent], axis=0),
        (((0,), (0,)), ((), ())),
        preferred_element_type=jnp.float32,
    )
    send_both = (row_scale[:, None] * picked_rows).astype(jnp.bfloat16)
    w_up_in = partner(w_up, "expert", 0)
    w_down_in = partner(w_down, "expert", 0)
    w_up_in, w_down_in, send_both, up_local, down_local = lax.optimization_barrier(
        (
            w_up_in,
            w_down_in,
            send_both,
            jnp.concatenate([m_up, v_up], axis=0),
            m_down,
        )
    )
    got_both = lax.all_to_all(
        send_both.reshape(experts, 2 * capacity, model_width),
        "expert",
        split_axis=0,
        concat_axis=0,
        tiled=True,
    )
    up_moments = partner(up_local, "expert", 0)
    v_down_in = partner(v_down, "expert", 0)
    w_up_use = jnp.where(swapped, w_up_in, w_up)
    w_down_use = jnp.where(swapped, w_down_in, w_down)
    up_full = lax.all_gather(w_up_use, "dp", axis=1, tiled=True)[0]
    down_full = lax.all_gather(w_down_use, "dp", axis=1, tiled=True)[0]
    slot_ids, buffer_ids = lax.optimization_barrier(
        (
            jnp.arange(row_total, dtype=jnp.int32),
            jnp.arange(2 * row_total, dtype=jnp.int32),
        )
    )
    token_at = (slot_ids // capacity) * (2 * capacity) + slot_ids % capacity
    take_token = (token_at[:, None] == buffer_ids[None, :]).astype(jnp.bfloat16)
    take_grad = (token_at[:, None] + capacity == buffer_ids[None, :]).astype(jnp.bfloat16)
    got_rows = got_both.reshape(2 * row_total, model_width)
    expert_rows = jnp.dot(take_token, got_rows, preferred_element_type=jnp.float32).astype(
        jnp.bfloat16
    )
    grad_rows = jnp.dot(take_grad, got_rows, preferred_element_type=jnp.float32).astype(
        jnp.bfloat16
    )
    up_act = jnp.dot(expert_rows, up_full, preferred_element_type=jnp.float32)
    hidden = jax.nn.silu(up_act).astype(jnp.bfloat16)
    down_full, hidden = lax.optimization_barrier((down_full, hidden))
    down_part = contract_rows(hidden, grad_rows).astype(jnp.bfloat16)
    down_part, up_moments, v_down_in, down_local = lax.optimization_barrier(
        (down_part, up_moments, v_down_in, down_local)
    )
    down_moments = partner(down_local, "expert", 0)
    expert_out = jnp.dot(hidden, down_full, preferred_element_type=jnp.float32).astype(jnp.bfloat16)
    hidden_grad = contract_cols(grad_rows, down_full)
    up_grad = (hidden_grad * silu_slope(up_act)).astype(jnp.bfloat16)
    input_part = contract_cols(up_grad, up_full).astype(jnp.bfloat16)
    input_part, down_moments = lax.optimization_barrier((input_part, down_moments))
    both_back = lax.all_to_all(
        (contract_rows(take_token, expert_out) + contract_rows(take_grad, input_part))
        .astype(jnp.bfloat16)
        .reshape(experts, 2 * capacity, model_width),
        "expert",
        split_axis=0,
        concat_axis=0,
        tiled=True,
    )
    up_gradient = lax.psum_scatter(
        contract_rows(expert_rows, up_grad).astype(jnp.bfloat16),
        "dp",
        scatter_dimension=0,
        tiled=True,
    ).astype(jnp.float32)
    down_gradient = lax.psum_scatter(
        down_part,
        "dp",
        scatter_dimension=0,
        tiled=True,
    ).astype(jnp.float32)
    m_up_use = jnp.where(swapped, up_moments[0:1], m_up)
    v_up_use = jnp.where(swapped, up_moments[1:2], v_up)
    m_down_use = jnp.where(swapped, down_moments, m_down)
    v_down_use = jnp.where(swapped, v_down_in, v_down)
    up_new = adam_update(w_up_use[0], m_up_use[0], v_up_use[0], up_gradient)
    down_new = adam_update(w_down_use[0], m_down_use[0], v_down_use[0], down_gradient)
    both_back, up_new, down_new = lax.optimization_barrier((both_back, up_new, down_new))
    back_rows = both_back.reshape(2 * row_total, model_width)
    out_hit = send_row[:, :, None] == row_ids[None, None, :]
    mixed = jnp.dot(
        jnp.sum(jnp.where(out_hit, gates[:, :, None], 0.0), axis=1),
        back_rows.astype(jnp.float32),
        precision=lax.Precision.HIGHEST,
        preferred_element_type=jnp.float32,
    ).astype(jnp.bfloat16)
    input_grad = jnp.dot(
        jnp.sum((send_row[:, :, None] + capacity == row_ids[None, None, :]).astype(
            jnp.bfloat16
        ), axis=1),
        back_rows,
        preferred_element_type=jnp.float32,
    ).astype(jnp.bfloat16)
    return (
        mixed,
        input_grad,
        up_new[0][None],
        down_new[0][None],
        up_new[1][None],
        up_new[2][None],
        down_new[1][None],
        down_new[2][None],
    )


def solution(mesh):
    return jax.shard_map(
        body,
        mesh=mesh,
        in_specs=(
            P(("dp", "expert"), None),
            P(("dp", "expert"), None),
            P(("dp", "expert"), None),
            P(("dp", "expert"), None),
            P(),
            P("expert", "dp", None),
            P("expert", "dp", None),
            P("expert", "dp", None),
            P("expert", "dp", None),
            P("expert", "dp", None),
            P("expert", "dp", None),
        ),
        out_specs=(
            P(("dp", "expert"), None),
            P(("dp", "expert"), None),
            P("expert", "dp", None),
            P("expert", "dp", None),
            P("expert", "dp", None),
            P("expert", "dp", None),
            P("expert", "dp", None),
            P("expert", "dp", None),
        ),
        check_vma=False,
    )
```

```python
import jax
import jax.numpy as jnp
from jax import lax
from jax.sharding import PartitionSpec as P

ADAM_STEP = 10


beta_one = 0.9
beta_two = 0.95
learn_rate = 0.001
adam_eps = 1e-08


def partner(value, axis, distance):
    mask = 2**distance
    pairs = [(source, source ^ mask) for source in range(lax.axis_size(axis))]
    return lax.ppermute(value, axis, pairs)


def silu_slope(value):
    sigma = jax.nn.sigmoid(value)
    return sigma * (1.0 + value * (1.0 - sigma))


def adam_update(weight, first_moment, second_moment, gradient):
    first_new = beta_one * first_moment.astype(jnp.float32) + (1.0 - beta_one) * gradient
    second_new = (
        beta_two * second_moment.astype(jnp.float32) + (1.0 - beta_two) * gradient * gradient
    )
    correct_one = 1.0 - beta_one**ADAM_STEP
    correct_two = 1.0 - beta_two**ADAM_STEP
    weight_new = weight.astype(jnp.float32) - learn_rate * (first_new / correct_one) / (
        jnp.sqrt(second_new / correct_two) + adam_eps
    )
    return (
        weight_new.astype(jnp.bfloat16),
        first_new.astype(jnp.bfloat16),
        second_new.astype(jnp.bfloat16),
    )


def contract_rows(left, right):
    return lax.dot_general(
        left, right, (((0,), (0,)), ((), ())), preferred_element_type=jnp.float32
    )


def contract_cols(left, right):
    return lax.dot_general(
        left, right, (((1,), (1,)), ((), ())), preferred_element_type=jnp.float32
    )


def stack_state(members):
    return jnp.stack([member.reshape(-1) for member in members])


def unstack_state(stacked, member_shapes):
    return tuple(
        (stacked[number].reshape(member_shape) for number, member_shape in enumerate(member_shapes))
    )


def body(tokens, routes, gates, cotangent, swap_flag, w_up, w_down, m_up, v_up, m_down, v_down):
    experts = lax.axis_size("expert")
    my_slot = lax.axis_index("expert")
    tok_count, model_width = tokens.shape
    chosen = routes.shape[1]
    pair_count = tok_count * chosen
    capacity = pair_count * 4 // (3 * experts)
    row_total = experts * capacity
    swapped = swap_flag[my_slot] == 1
    expert_ids = jnp.arange(experts, dtype=jnp.int32)
    route_hot = (routes.reshape(pair_count)[:, None] == expert_ids[None, :]).astype(jnp.int32)
    paired_hot = route_hot.reshape(pair_count, experts // 2, 2)[:, :, ::-1].reshape(
        pair_count, experts
    )
    dest_hot = jnp.where(swap_flag[None, :] == 1, paired_hot, route_hot)
    position = jnp.sum(jnp.cumsum(dest_hot, axis=0) * dest_hot, axis=1) - 1
    dest = jnp.sum(dest_hot * expert_ids[None, :], axis=1)
    send_row = (dest * (2 * capacity) + position).reshape(tok_count, chosen)
    row_ids = jnp.arange(2 * row_total, dtype=jnp.int32)
    token_pick = jnp.sum(
        (send_row[:, :, None] == row_ids[None, None, :]).astype(jnp.bfloat16), axis=1
    )
    grad_pick = jnp.sum(
        (send_row[:, :, None] + capacity == row_ids[None, None, :]).astype(jnp.bfloat16), axis=1
    )
    row_scale = jnp.sum(
        jnp.where(
            send_row[:, :, None] + capacity == row_ids[None, None, :], gates[:, :, None], 0.0
        ),
        axis=(0, 1),
    ) + jnp.sum(token_pick.astype(jnp.float32), axis=0)
    picked_rows = lax.dot_general(
        jnp.concatenate([token_pick, grad_pick], axis=0),
        jnp.concatenate([tokens, cotangent], axis=0),
        (((0,), (0,)), ((), ())),
        preferred_element_type=jnp.float32,
    )
    send_both = (row_scale[:, None] * picked_rows).astype(jnp.bfloat16)
    w_up_in = partner(w_up, "expert", 0)
    w_down_in = partner(w_down, "expert", 0)
    w_up_in, w_down_in, send_both, up_local, down_local = lax.optimization_barrier(
        (
            w_up_in,
            w_down_in,
            send_both,
            jnp.concatenate([m_up, v_up], axis=0),
            m_down,
        )
    )
    got_both = lax.all_to_all(
        send_both.reshape(experts, 2 * capacity, model_width),
        "expert",
        split_axis=0,
        concat_axis=0,
        tiled=True,
    )
    up_moments = partner(up_local, "expert", 0)
    v_down_in = partner(v_down, "expert", 0)
    w_up_use = jnp.where(swapped, w_up_in, w_up)
    w_down_use = jnp.where(swapped, w_down_in, w_down)
    up_full = lax.all_gather(w_up_use, "dp", axis=1, tiled=True)[0]
    down_full = lax.all_gather(w_down_use, "dp", axis=1, tiled=True)[0]
    slot_ids, buffer_ids = lax.optimization_barrier(
        (
            jnp.arange(row_total, dtype=jnp.int32),
            jnp.arange(2 * row_total, dtype=jnp.int32),
        )
    )
    token_at = (slot_ids // capacity) * (2 * capacity) + slot_ids % capacity
    take_token = (token_at[:, None] == buffer_ids[None, :]).astype(jnp.bfloat16)
    take_grad = (token_at[:, None] + capacity == buffer_ids[None, :]).astype(jnp.bfloat16)
    got_rows = got_both.reshape(2 * row_total, model_width)
    expert_rows = jnp.dot(take_token, got_rows, preferred_element_type=jnp.float32).astype(
        jnp.bfloat16
    )
    grad_rows = jnp.dot(take_grad, got_rows, preferred_element_type=jnp.float32).astype(
        jnp.bfloat16
    )
    up_act = jnp.dot(expert_rows, up_full, preferred_element_type=jnp.float32)
    hidden = jax.nn.silu(up_act).astype(jnp.bfloat16)
    down_full, hidden = lax.optimization_barrier((down_full, hidden))
    down_part = contract_rows(hidden, grad_rows).astype(jnp.bfloat16)
    down_part, up_moments, v_down_in, down_local = lax.optimization_barrier(
        (down_part, up_moments, v_down_in, down_local)
    )
    down_moments = partner(down_local, "expert", 0)
    expert_out = jnp.dot(hidden, down_full, preferred_element_type=jnp.float32).astype(jnp.bfloat16)
    hidden_grad = contract_cols(grad_rows, down_full)
    up_grad = (hidden_grad * silu_slope(up_act)).astype(jnp.bfloat16)
    input_part = contract_cols(up_grad, up_full).astype(jnp.bfloat16)
    out_rows = contract_rows(take_token, expert_out).astype(jnp.bfloat16)
    input_part, down_moments, out_rows = lax.optimization_barrier(
        (input_part, down_moments, out_rows)
    )
    both_back = lax.all_to_all(
        (out_rows.astype(jnp.float32) + contract_rows(take_grad, input_part))
        .astype(jnp.bfloat16)
        .reshape(experts, 2 * capacity, model_width),
        "expert",
        split_axis=0,
        concat_axis=0,
        tiled=True,
    )
    up_gradient = lax.psum_scatter(
        contract_rows(expert_rows, up_grad).astype(jnp.bfloat16),
        "dp",
        scatter_dimension=0,
        tiled=True,
    ).astype(jnp.float32)
    down_gradient = lax.psum_scatter(
        down_part,
        "dp",
        scatter_dimension=0,
        tiled=True,
    ).astype(jnp.float32)
    m_up_use = jnp.where(swapped, up_moments[0:1], m_up)
    v_up_use = jnp.where(swapped, up_moments[1:2], v_up)
    m_down_use = jnp.where(swapped, down_moments, m_down)
    v_down_use = jnp.where(swapped, v_down_in, v_down)
    up_new = adam_update(w_up_use[0], m_up_use[0], v_up_use[0], up_gradient)
    down_new = adam_update(w_down_use[0], m_down_use[0], v_down_use[0], down_gradient)
    both_back, up_new, down_new = lax.optimization_barrier((both_back, up_new, down_new))
    back_rows = both_back.reshape(2 * row_total, model_width)
    out_hit = send_row[:, :, None] == row_ids[None, None, :]
    mixed = jnp.dot(
        jnp.sum(jnp.where(out_hit, gates[:, :, None], 0.0), axis=1),
        back_rows.astype(jnp.float32),
        precision=lax.Precision.HIGHEST,
        preferred_element_type=jnp.float32,
    ).astype(jnp.bfloat16)
    input_grad = jnp.dot(
        jnp.sum((send_row[:, :, None] + capacity == row_ids[None, None, :]).astype(
            jnp.bfloat16
        ), axis=1),
        back_rows,
        preferred_element_type=jnp.float32,
    ).astype(jnp.bfloat16)
    return (
        mixed,
        input_grad,
        up_new[0][None],
        down_new[0][None],
        up_new[1][None],
        up_new[2][None],
        down_new[1][None],
        down_new[2][None],
    )


def solution(mesh):
    return jax.shard_map(
        body,
        mesh=mesh,
        in_specs=(
            P(("dp", "expert"), None),
            P(("dp", "expert"), None),
            P(("dp", "expert"), None),
            P(("dp", "expert"), None),
            P(),
            P("expert", "dp", None),
            P("expert", "dp", None),
            P("expert", "dp", None),
            P("expert", "dp", None),
            P("expert", "dp", None),
            P("expert", "dp", None),
        ),
        out_specs=(
            P(("dp", "expert"), None),
            P(("dp", "expert"), None),
            P("expert", "dp", None),
            P("expert", "dp", None),
            P("expert", "dp", None),
            P("expert", "dp", None),
            P("expert", "dp", None),
            P("expert", "dp", None),
        ),
        check_vma=False,
    )
```
